32 devices in a mesh: grp: 2 (over y), shot: 4 (over x, core), cable: 4 (over z).
Axes of the slice: x: 2, y: 2, z: 4, core: 2. Of those that a mesh axis runs over, the one named last changes fastest.
Arguments:
- features: bfloat16 [4, 128, 32, 8, 128], P('cable', None, ('grp', 'shot')), parts along dimension 2, may hold values from -6 to 6
- counts: int32 [32, 4], P('grp', 'cable'), parts along dimension 0, may hold values from 64 to 128, as said below
- first_weight: bfloat16 [5, 3, 5, 64, 64], replicated, may hold values from -0.09375 to 0.09375
- second_weight: bfloat16 [5, 3, 5, 64, 64], replicated, may hold values from -0.09375 to 0.09375
Outputs:
- denoised: bfloat16 [4, 128, 32, 8, 128], P('cable', 'shot', 'grp'), parts along dimension 2
The draws below stay inside these ranges and needn't reach their ends.
There are 2 independent parts, one for each index of `grp`. The reference program is written for one: setup_inputs(seed, part) draws one part's arguments, and reference() takes and returns one part's arrays. A program takes and returns all parts, laid end to end along the dimension named above; an argument that names none is the same for every part. Nothing has to cross between parts.
Inputs may be any that keep to these rules, and one draw needn't show every extreme that they name: counts[s, c] is the number of live receivers of streamer c in shot s; receivers j < counts[s, c] are live; in every draw some gather has all 128 receivers live.
All inputs are finite; a program needn't handle non-finite values.
Results may differ from the reference program's by a relative error of at most 0.003.
Values may be sent and summed in bfloat16 or wider, within the bound.
No kernel may reach another device: no remote copies, remote signals or barrier semaphores. Data moves between devices by JAX's collectives and lax.ppermute only.
A program may use at most 128 MiB of HBM per device.

```python
import jax
import jax.numpy as jnp
from jax import lax

C = 64
NT = 16
RD = 128
NCAB = 4
S = 16
NTP = 8


def draw_counts(key, part):
    first_key, second_key = jax.random.split(key)
    counted = jax.random.randint(first_key, (S * NCAB,), RD // 2, RD + 1, dtype=jnp.int32)
    full_spot = jax.random.randint(second_key, (), 0, S * NCAB, dtype=jnp.int32)
    counted = counted.at[full_spot].set(RD)
    return counted.reshape(S, NCAB)


def block_levels(rng, dims, pieces, smallest, largest):
    loudness = 1.0
    for dim, blocks in pieces:
        steps = jax.random.uniform(jax.random.fold_in(jax.random.fold_in(rng, 6), dim), (blocks,), jnp.float32, smallest / len(pieces), largest / len(pieces))
        loudness = loudness * jnp.repeat(jnp.exp(steps), dims[dim] // blocks).reshape((-1,) + (1,) * (len(dims) - 1 - dim))
    return loudness


def gaussian(rng, shape, scale, bound, cuts=(), kind=jnp.bfloat16):
    entries = scale * jax.random.normal(rng, shape, jnp.float32)
    if cuts:
        entries = entries * block_levels(rng, shape, cuts, -0.22, 0.18)
    return jnp.clip(entries, -bound, bound).astype(kind)


def setup_inputs(seed: int = 0, part: int = 0) -> dict:
    keys = jax.random.split(jax.random.key(seed), 5)
    part_splits = jax.random.split(jax.random.fold_in(keys[4], part), 5)
    features = gaussian(part_splits[0], (NCAB, RD, S, NTP, 2 * C), 1.0, 6.0, ((0, 4), (2, 4)))
    counts = draw_counts(jax.random.fold_in(jax.random.fold_in(keys[4], part), 71), part)
    first_weight = gaussian(keys[2], (5, 3, 5, C, C), (75 * C) ** -0.5, 0.09375)
    second_weight = gaussian(keys[3], (5, 3, 5, C, C), (75 * C) ** -0.5, 0.09375)
    return {"features": features, "counts": counts, "first_weight": first_weight, "second_weight": second_weight}


def conv_layer(cable_block, weight, dilation, alive_mask):
    convolved = lax.conv_general_dilated(
        cable_block[None],
        weight.astype(jnp.float32),
        window_strides=(1, 1, 1),
        padding=((2 * dilation, 2 * dilation), (1, 1), (2, 2)),
        rhs_dilation=(dilation, 1, 1),
        dimension_numbers=("NDHWC", "DHWIO", "NDHWC"),
        precision=lax.Precision.HIGHEST,
    )[0]
    return (alive_mask * (cable_block + jnp.maximum(convolved, 0.0))).astype(jnp.bfloat16)


def reference(features, counts, first_weight, second_weight):
    natural = features.reshape(NCAB, RD, S, NT, C)
    receiver_ids = jnp.arange(RD, dtype=jnp.int32)
    live_table = (receiver_ids[None, :, None] < counts.T[:, None, :]).astype(jnp.float32)

    def per_cable(members):
        cable_block, alive_flat = members
        alive_mask = alive_flat[:, :, None, None]
        masked = alive_mask * cable_block.astype(jnp.float32)
        hidden = conv_layer(masked, first_weight, 1, alive_mask)
        return conv_layer(hidden.astype(jnp.float32), second_weight, 4, alive_mask)

    denoised = lax.map(per_cable, (natural, live_table))
    return denoised.reshape(NCAB, RD, S, NTP, 2 * C)
```

```python
import functools

import jax
import jax.numpy as jnp
from jax import lax
from jax.experimental import pallas as pl
from jax.experimental.pallas import tpu as pltpu
from jax.sharding import PartitionSpec as P


def extended(block, axis, dim, width):
    count = lax.axis_size(axis)
    forward = [(i, i + 1) for i in range(count - 1)]
    backward = [(target, source) for source, target in forward]
    low = lax.ppermute(
        lax.slice_in_dim(block, block.shape[dim] - width, None, axis=dim), axis, forward
    )
    high = lax.ppermute(lax.slice_in_dim(block, 0, width, axis=dim), axis, backward)
    return jnp.concatenate([low, block, high], axis=dim)


def pair_weights(weight):
    channels = weight.shape[3]
    zeroed = jnp.zeros(weight.shape[:2] + (channels, channels), weight.dtype)
    row_blocks = []
    for time_step in range(3):
        for in_phase in range(2):
            column_blocks = []
            for out_phase in range(2):
                tap_time = 2 * time_step + in_phase - out_phase
                if 0 <= tap_time <= 4:
                    column_blocks.append(weight[:, :, tap_time])
                else:
                    column_blocks.append(zeroed)
            row_blocks.append(jnp.concatenate(column_blocks, axis=3))
    stacked = jnp.concatenate(row_blocks, axis=2)
    return stacked.reshape((-1,) + stacked.shape[2:])


def stack_time(block, dilation):
    pairs = block.shape[2]
    padded = jnp.pad(block, ((0, 0), (2 * dilation, 2 * dilation), (1, 1), (0, 0)))
    stacked = jnp.concatenate(
        [padded[:, :, 0:pairs], padded[:, :, 1 : pairs + 1], padded[:, :, 2 : pairs + 2]],
        axis=3,
    )
    return stacked.reshape(stacked.shape[0], -1, stacked.shape[3])


def conv_kernel(counts_ref, xs_ref, w_ref, res_ref, out_ref, acc_ref, *, dilation, pairs):
    s = pl.program_id(0)
    rows = acc_ref.shape[0]
    for a in range(5):
        for b in range(3):
            lhs = xs_ref[s + b, pl.ds(a * dilation * pairs, rows), :]
            contrib = jnp.dot(lhs, w_ref[a * 3 + b], preferred_element_type=jnp.float32)
            if a == 0 and b == 0:
                acc_ref[...] = contrib
            else:
                acc_ref[...] += contrib
    receiver = lax.broadcasted_iota(jnp.int32, acc_ref.shape, 0) // pairs
    live = receiver < counts_ref[s]
    value = res_ref[0].astype(jnp.float32) + jnp.maximum(acc_ref[...], 0.0)
    out_ref[0] = jnp.where(live, value, 0.0).astype(out_ref.dtype)


def conv_layer(counts, bordered, residual, weights, dilation):
    shots, receivers, pairs, lanes = residual.shape
    rows = receivers * pairs
    xs = stack_time(bordered, dilation)
    flat = residual.reshape(shots, rows, lanes)
    out = pl.pallas_call(
        functools.partial(conv_kernel, dilation=dilation, pairs=pairs),
        grid_spec=pltpu.PrefetchScalarGridSpec(
            num_scalar_prefetch=1,
            grid=(shots,),
            in_specs=[
                pl.BlockSpec(xs.shape, lambda s, c: (0, 0, 0)),
                pl.BlockSpec(weights.shape, lambda s, c: (0, 0, 0)),
                pl.BlockSpec((1, rows, lanes), lambda s, c: (s, 0, 0)),
            ],
            out_specs=pl.BlockSpec((1, rows, lanes), lambda s, c: (s, 0, 0)),
            scratch_shapes=[pltpu.VMEM((rows, lanes), jnp.float32)],
        ),
        out_shape=jax.ShapeDtypeStruct((shots, rows, lanes), jnp.bfloat16),
        compiler_params=pltpu.CompilerParams(vmem_limit_bytes=48 * 1024 * 1024),
    )(counts, xs, weights, flat)
    return out.reshape(shots, receivers, pairs, lanes)


def body(features, counts, first_weight, second_weight):
    receivers = features.shape[1]
    shot_local = features.shape[2]
    shot_index = lax.axis_index("shot")
    chosen = lax.dynamic_slice_in_dim(counts[:, 0], shot_index * shot_local, shot_local)
    first_pairs = pair_weights(first_weight)
    second_pairs = pair_weights(second_weight)
    volume = jnp.transpose(features[0], (1, 0, 2, 3))
    alive = jnp.arange(receivers, dtype=jnp.int32)[None, :] < chosen[:, None]
    inputs = volume * alive.astype(volume.dtype)[:, :, None, None]
    bordered = extended(inputs, "shot", 0, 1)
    hidden = conv_layer(chosen, bordered, inputs, first_pairs, 1)
    edged = extended(hidden, "shot", 0, 1)
    result = conv_layer(chosen, edged, hidden, second_pairs, 4)
    moved = lax.all_to_all(result, "shot", split_axis=1, concat_axis=0, tiled=True)
    return jnp.transpose(moved, (1, 0, 2, 3))[None]


def solution(mesh):
    placed = (P("cable", None, ("grp", "shot"), None, None), P("grp", "cable"), P(), P())
    return jax.shard_map(
        body,
        mesh=mesh,
        in_specs=placed,
        out_specs=P("cable", "shot", "grp", None, None),
        check_vma=False,
    )
```

```python
import functools

import jax
import jax.numpy as jnp
from jax import lax
from jax.experimental import pallas as pl
from jax.experimental.pallas import tpu as pltpu
from jax.sharding import PartitionSpec as P


def extended(block, axis, dim, width):
    count = lax.axis_size(axis)
    forward = [(i, i + 1) for i in range(count - 1)]
    backward = [(target, source) for source, target in forward]
    low = lax.ppermute(
        lax.slice_in_dim(block, block.shape[dim] - width, None, axis=dim), axis, forward
    )
    high = lax.ppermute(lax.slice_in_dim(block, 0, width, axis=dim), axis, backward)
    return jnp.concatenate([low, block, high], axis=dim)


def pair_weights(weight):
    channels = weight.shape[3]
    zeroed = jnp.zeros(weight.shape[:2] + (channels, channels), weight.dtype)
    row_blocks = []
    for time_step in range(3):
        for in_phase in range(2):
            column_blocks = []
            for out_phase in range(2):
                tap_time = 2 * time_step + in_phase - out_phase
                if 0 <= tap_time <= 4:
                    column_blocks.append(weight[:, :, tap_time])
                else:
                    column_blocks.append(zeroed)
            row_blocks.append(jnp.concatenate(column_blocks, axis=3))
    stacked = jnp.concatenate(row_blocks, axis=2)
    return stacked.reshape((-1,) + stacked.shape[2:])


def stack_time(block, dilation):
    pairs = block.shape[2]
    padded = jnp.pad(block, ((0, 0), (2 * dilation, 2 * dilation), (1, 1), (0, 0)))
    stacked = jnp.concatenate(
        [padded[:, :, 0:pairs], padded[:, :, 1 : pairs + 1], padded[:, :, 2 : pairs + 2]],
        axis=3,
    )
    return stacked.reshape(stacked.shape[0], -1, stacked.shape[3])


def conv_kernel(scalars_ref, xs_ref, w_ref, res_ref, out_ref, acc_ref, *, dilation, pairs):
    s = pl.program_id(0)
    rows = acc_ref.shape[0]
    for a in range(5):
        for b in range(3):
            lhs = xs_ref[s + b, pl.ds(a * dilation * pairs, rows), :]
            contrib = jnp.dot(lhs, w_ref[a * 3 + b], preferred_element_type=jnp.float32)
            if a == 0 and b == 0:
                acc_ref[...] = contrib
            else:
                acc_ref[...] += contrib
    first = scalars_ref[0] * (rows // pairs)
    receiver = first + lax.broadcasted_iota(jnp.int32, acc_ref.shape, 0) // pairs
    live = receiver < scalars_ref[1 + s]
    value = res_ref[0].astype(jnp.float32) + jnp.maximum(acc_ref[...], 0.0)
    out_ref[0] = jnp.where(live, value, 0.0).astype(out_ref.dtype)


def conv_call(xs, weights, flat, counts, dilation, pairs, block, block_rows):
    shots, _, lanes = flat.shape
    window = block_rows + 4 * dilation * pairs
    scalars = jnp.concatenate([jnp.reshape(block, (1,)).astype(jnp.int32), counts])
    flops = 2 * shots * 15 * block_rows * xs.shape[2] * lanes
    return pl.pallas_call(
        functools.partial(conv_kernel, dilation=dilation, pairs=pairs),
        grid_spec=pltpu.PrefetchScalarGridSpec(
            num_scalar_prefetch=1,
            grid=(shots,),
            in_specs=[
                pl.BlockSpec(
                    (pl.Element(xs.shape[0]), pl.Element(window), pl.Element(xs.shape[2])),
                    lambda s, c: (0, c[0] * block_rows, 0),
                ),
                pl.BlockSpec(weights.shape, lambda s, c: (0, 0, 0)),
                pl.BlockSpec((1, block_rows, lanes), lambda s, c: (s, c[0], 0)),
            ],
            out_specs=pl.BlockSpec((1, block_rows, lanes), lambda s, c: (s, 0, 0)),
            scratch_shapes=[pltpu.VMEM((block_rows, lanes), jnp.float32)],
        ),
        out_shape=jax.ShapeDtypeStruct((shots, block_rows, lanes), jnp.bfloat16),
        compiler_params=pltpu.CompilerParams(vmem_limit_bytes=48 * 1024 * 1024),
        cost_estimate=pl.CostEstimate(
            flops=flops,
            transcendentals=0,
            bytes_accessed=xs.shape[0] * window * xs.shape[2] * 2 + weights.size * 2
            + 4 * shots * block_rows * lanes,
        ),
    )(scalars, xs, weights, flat)


def body(features, counts, first_weight, second_weight):
    receivers = features.shape[1]
    shot_local = features.shape[2]
    pairs = features.shape[3]
    lanes = features.shape[4]
    count = lax.axis_size("shot")
    me = lax.axis_index("shot")
    chosen = lax.dynamic_slice_in_dim(counts[:, 0], me * shot_local, shot_local)
    first_pairs = pair_weights(first_weight)
    second_pairs = pair_weights(second_weight)
    volume = jnp.transpose(features[0], (1, 0, 2, 3))
    alive = jnp.arange(receivers, dtype=jnp.int32)[None, :] < chosen[:, None]
    inputs = volume * alive.astype(volume.dtype)[:, :, None, None]
    bordered = extended(inputs, "shot", 0, 1)
    xs1 = stack_time(bordered, 1)
    flat1 = inputs.reshape(shot_local, receivers * pairs, lanes)
    hidden = conv_call(xs1, first_pairs, flat1, chosen, 1, pairs, 0, receivers * pairs)
    hidden = hidden.reshape(shot_local, receivers, pairs, lanes)
    edged = extended(hidden, "shot", 0, 1)
    xs2 = stack_time(edged, 4)
    flat2 = hidden.reshape(shot_local, receivers * pairs, lanes)
    span = receivers // count
    arrived = []
    for shift in list(range(1, count)) + [0]:
        target = lax.rem(me + shift, count)
        piece = conv_call(xs2, second_pairs, flat2, chosen, 4, pairs, target, span * pairs)
        if shift:
            pairs_list = [(i, (i + shift) % count) for i in range(count)]
            piece = lax.ppermute(piece, "shot", pairs_list)
        arrived.append((shift, piece))
    by_shift = jnp.stack([piece for _, piece in sorted(arrived, key=lambda t: t[0])])
    order = lax.rem(me - jnp.arange(count, dtype=jnp.int32) + count, count)
    ordered = jnp.take(by_shift, order, axis=0)
    ordered = ordered.reshape(count * shot_local, span, pairs, lanes)
    return jnp.transpose(ordered, (1, 0, 2, 3))[None]


def solution(mesh):
    placed = (P("cable", None, ("grp", "shot"), None, None), P("grp", "cable"), P(), P())
    return jax.shard_map(
        body,
        mesh=mesh,
        in_specs=placed,
        out_specs=P("cable", "shot", "grp", None, None),
        check_vma=False,
    )
```

```python
import functools

import jax
import jax.numpy as jnp
from jax import lax
from jax.experimental import pallas as pl
from jax.experimental.pallas import tpu as pltpu
from jax.sharding import PartitionSpec as P


def extended(block, axis, dim, width):
    count = lax.axis_size(axis)
    forward = [(i, i + 1) for i in range(count - 1)]
    backward = [(target, source) for source, target in forward]
    low = lax.ppermute(
        lax.slice_in_dim(block, block.shape[dim] - width, None, axis=dim), axis, forward
    )
    high = lax.ppermute(lax.slice_in_dim(block, 0, width, axis=dim), axis, backward)
    return jnp.concatenate([low, block, high], axis=dim)


def pair_weights(weight):
    channels = weight.shape[3]
    zeroed = jnp.zeros(weight.shape[:2] + (channels, channels), weight.dtype)
    row_blocks = []
    for time_step in range(3):
        for in_phase in range(2):
            column_blocks = []
            for out_phase in range(2):
                tap_time = 2 * time_step + in_phase - out_phase
                if 0 <= tap_time <= 4:
                    column_blocks.append(weight[:, :, tap_time])
                else:
                    column_blocks.append(zeroed)
            row_blocks.append(jnp.concatenate(column_blocks, axis=3))
    stacked = jnp.concatenate(row_blocks, axis=2)
    return stacked.reshape((-1,) + stacked.shape[2:])


def stack_time(block, dilation):
    pairs = block.shape[2]
    padded = jnp.pad(block, ((0, 0), (2 * dilation, 2 * dilation), (1, 1), (0, 0)))
    stacked = jnp.concatenate(
        [padded[:, :, 0:pairs], padded[:, :, 1 : pairs + 1], padded[:, :, 2 : pairs + 2]],
        axis=3,
    )
    return stacked.reshape(stacked.shape[0], -1, stacked.shape[3])


def spread_call(xs, weights, flat, counts, dilation, pairs):
    shots, rows, lanes = flat.shape
    scalars = jnp.concatenate([jnp.zeros((1,), jnp.int32), counts])
    flops = 2 * shots * 15 * xs.shape[1] * xs.shape[2] * weights.shape[2]
    return pl.pallas_call(
        functools.partial(spread_kernel, dilation=dilation, pairs=pairs),
        grid_spec=pltpu.PrefetchScalarGridSpec(
            num_scalar_prefetch=1,
            grid=(shots,),
            in_specs=[
                pl.BlockSpec(xs.shape, lambda s, c: (0, 0, 0)),
                pl.BlockSpec(weights.shape, lambda s, c: (0, 0, 0)),
                pl.BlockSpec((1, rows, lanes), lambda s, c: (s, 0, 0)),
            ],
            out_specs=pl.BlockSpec((1, rows, lanes), lambda s, c: (s, 0, 0)),
        ),
        out_shape=jax.ShapeDtypeStruct((shots, rows, lanes), jnp.bfloat16),
        compiler_params=pltpu.CompilerParams(vmem_limit_bytes=48 * 1024 * 1024),
        cost_estimate=pl.CostEstimate(
            flops=flops,
            transcendentals=0,
            bytes_accessed=xs.size * 2 + weights.size * 2 + 4 * shots * rows * lanes,
        ),
    )(scalars, xs, weights, flat)


def spread_kernel(scalars_ref, xs_ref, w_ref, res_ref, out_ref, *, dilation, pairs):
    s = pl.program_id(0)
    rows, lanes = out_ref.shape[1:]
    total = None
    for b in range(3):
        taps = jnp.concatenate([w_ref[a * 3 + b] for a in range(5)], axis=1)
        spread = jnp.dot(xs_ref[s + b], taps, preferred_element_type=jnp.float32)
        for a in range(5):
            part = spread[a * dilation * pairs : a * dilation * pairs + rows, a * lanes : (a + 1) * lanes]
            total = part if total is None else total + part
    first = scalars_ref[0] * (rows // pairs)
    receiver = first + lax.broadcasted_iota(jnp.int32, (rows, lanes), 0) // pairs
    live = receiver < scalars_ref[1 + s]
    value = res_ref[0].astype(jnp.float32) + jnp.maximum(total, 0.0)
    out_ref[0] = jnp.where(live, value, 0.0).astype(out_ref.dtype)


def conv_kernel(scalars_ref, xs_ref, w_ref, res_ref, out_ref, acc_ref, *, dilation, pairs):
    s = pl.program_id(0)
    rows = acc_ref.shape[0]
    for a in range(5):
        for b in range(3):
            lhs = xs_ref[s + b, pl.ds(a * dilation * pairs, rows), :]
            contrib = jnp.dot(lhs, w_ref[a * 3 + b], preferred_element_type=jnp.float32)
            if a == 0 and b == 0:
                acc_ref[...] = contrib
            else:
                acc_ref[...] += contrib
    first = scalars_ref[0] * (rows // pairs)
    receiver = first + lax.broadcasted_iota(jnp.int32, acc_ref.shape, 0) // pairs
    live = receiver < scalars_ref[1 + s]
    value = res_ref[0].astype(jnp.float32) + jnp.maximum(acc_ref[...], 0.0)
    out_ref[0] = jnp.where(live, value, 0.0).astype(out_ref.dtype)


def conv_call(xs, weights, flat, counts, dilation, pairs, block, block_rows):
    shots, _, lanes = flat.shape
    window = block_rows + 4 * dilation * pairs
    scalars = jnp.concatenate([jnp.reshape(block, (1,)).astype(jnp.int32), counts])
    flops = 2 * shots * 15 * block_rows * xs.shape[2] * lanes
    return pl.pallas_call(
        functools.partial(conv_kernel, dilation=dilation, pairs=pairs),
        grid_spec=pltpu.PrefetchScalarGridSpec(
            num_scalar_prefetch=1,
            grid=(shots,),
            in_specs=[
                pl.BlockSpec(
                    (pl.Element(xs.shape[0]), pl.Element(window), pl.Element(xs.shape[2])),
                    lambda s, c: (0, c[0] * block_rows, 0),
                ),
                pl.BlockSpec(weights.shape, lambda s, c: (0, 0, 0)),
                pl.BlockSpec((1, block_rows, lanes), lambda s, c: (s, c[0], 0)),
            ],
            out_specs=pl.BlockSpec((1, block_rows, lanes), lambda s, c: (s, 0, 0)),
            scratch_shapes=[pltpu.VMEM((block_rows, lanes), jnp.float32)],
        ),
        out_shape=jax.ShapeDtypeStruct((shots, block_rows, lanes), jnp.bfloat16),
        compiler_params=pltpu.CompilerParams(vmem_limit_bytes=48 * 1024 * 1024),
        cost_estimate=pl.CostEstimate(
            flops=flops,
            transcendentals=0,
            bytes_accessed=xs.shape[0] * window * xs.shape[2] * 2 + weights.size * 2
            + 4 * shots * block_rows * lanes,
        ),
    )(scalars, xs, weights, flat)


def body(features, counts, first_weight, second_weight):
    receivers = features.shape[1]
    shot_local = features.shape[2]
    pairs = features.shape[3]
    lanes = features.shape[4]
    count = lax.axis_size("shot")
    me = lax.axis_index("shot")
    chosen = lax.dynamic_slice_in_dim(counts[:, 0], me * shot_local, shot_local)
    first_pairs = pair_weights(first_weight)
    second_pairs = pair_weights(second_weight)
    volume = jnp.transpose(features[0], (1, 0, 2, 3))
    alive = jnp.arange(receivers, dtype=jnp.int32)[None, :] < chosen[:, None]
    inputs = volume * alive.astype(volume.dtype)[:, :, None, None]
    bordered = extended(inputs, "shot", 0, 1)
    xs1 = stack_time(bordered, 1)
    flat1 = inputs.reshape(shot_local, receivers * pairs, lanes)
    hidden = spread_call(xs1, first_pairs, flat1, chosen, 1, pairs)
    hidden = hidden.reshape(shot_local, receivers, pairs, lanes)
    edged = extended(hidden, "shot", 0, 1)
    xs2 = stack_time(edged, 4)
    flat2 = hidden.reshape(shot_local, receivers * pairs, lanes)
    span = receivers // count
    arrived = []
    for shift in list(range(1, count)) + [0]:
        target = lax.rem(me + shift, count)
        piece = conv_call(xs2, second_pairs, flat2, chosen, 4, pairs, target, span * pairs)
        if shift:
            pairs_list = [(i, (i + shift) % count) for i in range(count)]
            piece = lax.ppermute(piece, "shot", pairs_list)
        arrived.append((shift, piece))
    by_shift = jnp.stack([piece for _, piece in sorted(arrived, key=lambda t: t[0])])
    order = lax.rem(me - jnp.arange(count, dtype=jnp.int32) + count, count)
    ordered = jnp.take(by_shift, order, axis=0)
    ordered = ordered.reshape(count * shot_local, span, pairs, lanes)
    return jnp.transpose(ordered, (1, 0, 2, 3))[None]


def solution(mesh):
    placed = (P("cable", None, ("grp", "shot"), None, None), P("grp", "cable"), P(), P())
    return jax.shard_map(
        body,
        mesh=mesh,
        in_specs=placed,
        out_specs=P("cable", "shot", "grp", None, None),
        check_vma=False,
    )
```

```python
import functools

import jax
import jax.numpy as jnp
from jax import lax
from jax.experimental import pallas as pl
from jax.experimental.pallas import tpu as pltpu
from jax.sharding import PartitionSpec as P


def extended(block, axis, dim, width):
    count = lax.axis_size(axis)
    forward = [(i, i + 1) for i in range(count - 1)]
    backward = [(target, source) for source, target in forward]
    low = lax.ppermute(
        lax.slice_in_dim(block, block.shape[dim] - width, None, axis=dim), axis, forward
    )
    high = lax.ppermute(lax.slice_in_dim(block, 0, width, axis=dim), axis, backward)
    return jnp.concatenate([low, block, high], axis=dim)


def pair_weights(weight):
    channels = weight.shape[3]
    zeroed = jnp.zeros(weight.shape[:2] + (channels, channels), weight.dtype)
    row_blocks = []
    for time_step in range(3):
        for in_phase in range(2):
            column_blocks = []
            for out_phase in range(2):
                tap_time = 2 * time_step + in_phase - out_phase
                if 0 <= tap_time <= 4:
                    column_blocks.append(weight[:, :, tap_time])
                else:
                    column_blocks.append(zeroed)
            row_blocks.append(jnp.concatenate(column_blocks, axis=3))
    stacked = jnp.concatenate(row_blocks, axis=2)
    return stacked.reshape((-1,) + stacked.shape[2:])


def stack_time(block, dilation):
    pairs = block.shape[2]
    padded = jnp.pad(block, ((0, 0), (2 * dilation, 2 * dilation), (1, 1), (0, 0)))
    stacked = jnp.concatenate(
        [padded[:, :, 0:pairs], padded[:, :, 1 : pairs + 1], padded[:, :, 2 : pairs + 2]],
        axis=3,
    )
    return stacked.reshape(stacked.shape[0], -1, stacked.shape[3])


def spread_call(xs, weights, flat, counts, dilation, pairs):
    shots, rows, lanes = flat.shape
    scalars = jnp.concatenate([jnp.zeros((1,), jnp.int32), counts])
    flops = 2 * shots * 15 * xs.shape[1] * xs.shape[2] * weights.shape[2]
    return pl.pallas_call(
        functools.partial(spread_kernel, dilation=dilation, pairs=pairs),
        grid_spec=pltpu.PrefetchScalarGridSpec(
            num_scalar_prefetch=1,
            grid=(shots,),
            in_specs=[
                pl.BlockSpec(xs.shape, lambda s, c: (0, 0, 0)),
                pl.BlockSpec(weights.shape, lambda s, c: (0, 0, 0)),
                pl.BlockSpec((1, rows, lanes), lambda s, c: (s, 0, 0)),
            ],
            out_specs=pl.BlockSpec((1, rows, lanes), lambda s, c: (s, 0, 0)),
        ),
        out_shape=jax.ShapeDtypeStruct((shots, rows, lanes), jnp.bfloat16),
        compiler_params=pltpu.CompilerParams(vmem_limit_bytes=48 * 1024 * 1024),
        cost_estimate=pl.CostEstimate(
            flops=flops,
            transcendentals=0,
            bytes_accessed=xs.size * 2 + weights.size * 2 + 4 * shots * rows * lanes,
        ),
    )(scalars, xs, weights, flat)


def spread_kernel(scalars_ref, xs_ref, w_ref, res_ref, out_ref, *, dilation, pairs):
    s = pl.program_id(0)
    rows, lanes = out_ref.shape[1:]
    total = None
    for b in range(3):
        taps = jnp.concatenate([w_ref[a * 3 + b] for a in range(5)], axis=1)
        spread = jnp.dot(xs_ref[s + b], taps, preferred_element_type=jnp.float32)
        for a in range(5):
            part = spread[a * dilation * pairs : a * dilation * pairs + rows, a * lanes : (a + 1) * lanes]
            total = part if total is None else total + part
    first = scalars_ref[0] * (rows // pairs)
    receiver = first + lax.broadcasted_iota(jnp.int32, (rows, lanes), 0) // pairs
    live = receiver < scalars_ref[1 + s]
    value = res_ref[0].astype(jnp.float32) + jnp.maximum(total, 0.0)
    out_ref[0] = jnp.where(live, value, 0.0).astype(out_ref.dtype)


def conv_kernel(scalars_ref, xs_ref, w_ref, res_ref, out_ref, acc_ref, *, dilation, pairs):
    s = pl.program_id(0)
    rows = acc_ref.shape[0]
    for a in range(5):
        for b in range(3):
            lhs = xs_ref[s + b, pl.ds(a * dilation * pairs, rows), :]
            contrib = jnp.dot(lhs, w_ref[a * 3 + b], preferred_element_type=jnp.float32)
            if a == 0 and b == 0:
                acc_ref[...] = contrib
            else:
                acc_ref[...] += contrib
    first = scalars_ref[0] * (rows // pairs)
    receiver = first + lax.broadcasted_iota(jnp.int32, acc_ref.shape, 0) // pairs
    live = receiver < scalars_ref[1 + s]
    value = res_ref[0].astype(jnp.float32) + jnp.maximum(acc_ref[...], 0.0)
    out_ref[0] = jnp.where(live, value, 0.0).astype(out_ref.dtype)


def conv_call(xs, weights, flat, counts, dilation, pairs, block, block_rows):
    shots, _, lanes = flat.shape
    window = block_rows + 4 * dilation * pairs
    scalars = jnp.concatenate([jnp.reshape(block, (1,)).astype(jnp.int32), counts])
    flops = 2 * shots * 15 * block_rows * xs.shape[2] * lanes
    return pl.pallas_call(
        functools.partial(conv_kernel, dilation=dilation, pairs=pairs),
        grid_spec=pltpu.PrefetchScalarGridSpec(
            num_scalar_prefetch=1,
            grid=(shots,),
            in_specs=[
                pl.BlockSpec(
                    (pl.Element(xs.shape[0]), pl.Element(window), pl.Element(xs.shape[2])),
                    lambda s, c: (0, c[0] * block_rows, 0),
                ),
                pl.BlockSpec(weights.shape, lambda s, c: (0, 0, 0)),
                pl.BlockSpec((1, block_rows, lanes), lambda s, c: (s, c[0], 0)),
            ],
            out_specs=pl.BlockSpec((1, block_rows, lanes), lambda s, c: (s, 0, 0)),
            scratch_shapes=[pltpu.VMEM((block_rows, lanes), jnp.float32)],
        ),
        out_shape=jax.ShapeDtypeStruct((shots, block_rows, lanes), jnp.bfloat16),
        compiler_params=pltpu.CompilerParams(vmem_limit_bytes=48 * 1024 * 1024),
        cost_estimate=pl.CostEstimate(
            flops=flops,
            transcendentals=0,
            bytes_accessed=xs.shape[0] * window * xs.shape[2] * 2 + weights.size * 2
            + 4 * shots * block_rows * lanes,
        ),
    )(scalars, xs, weights, flat)


def body(features, counts, first_weight, second_weight):
    receivers = features.shape[1]
    shot_local = features.shape[2]
    pairs = features.shape[3]
    lanes = features.shape[4]
    count = lax.axis_size("shot")
    me = lax.axis_index("shot")
    chosen = lax.dynamic_slice_in_dim(counts[:, 0], me * shot_local, shot_local)
    first_pairs = pair_weights(first_weight)
    second_pairs = pair_weights(second_weight)
    volume = jnp.transpose(features[0], (1, 0, 2, 3))
    alive = jnp.arange(receivers, dtype=jnp.int32)[None, :] < chosen[:, None]
    inputs = volume * alive.astype(volume.dtype)[:, :, None, None]
    bordered = extended(inputs, "shot", 0, 1)
    xs1 = stack_time(bordered, 1)
    flat1 = inputs.reshape(shot_local, receivers * pairs, lanes)
    hidden = spread_call(xs1, first_pairs, flat1, chosen, 1, pairs)
    hidden = hidden.reshape(shot_local, receivers, pairs, lanes)
    edged = extended(hidden, "shot", 0, 1)
    xs2 = stack_time(edged, 4)
    flat2 = hidden.reshape(shot_local, receivers * pairs, lanes)
    span = receivers // count
    whole = spread_call(xs2, second_pairs, flat2, chosen, 4, pairs)
    arrived = []
    for shift in range(count):
        target = lax.rem(me + shift, count)
        piece = lax.dynamic_slice_in_dim(whole, target * span * pairs, span * pairs, axis=1)
        if shift:
            pairs_list = [(i, (i + shift) % count) for i in range(count)]
            piece = lax.ppermute(piece, "shot", pairs_list)
        arrived.append((shift, piece))
    by_shift = jnp.stack([piece for _, piece in sorted(arrived, key=lambda t: t[0])])
    order = lax.rem(me - jnp.arange(count, dtype=jnp.int32) + count, count)
    ordered = jnp.take(by_shift, order, axis=0)
    ordered = ordered.reshape(count * shot_local, span, pairs, lanes)
    return jnp.transpose(ordered, (1, 0, 2, 3))[None]


def solution(mesh):
    placed = (P("cable", None, ("grp", "shot"), None, None), P("grp", "cable"), P(), P())
    return jax.shard_map(
        body,
        mesh=mesh,
        in_specs=placed,
        out_specs=P("cable", "shot", "grp", None, None),
        check_vma=False,
    )
```

```python
import functools

import jax
import jax.numpy as jnp
from jax import lax
from jax.experimental import pallas as pl
from jax.experimental.pallas import tpu as pltpu
from jax.sharding import PartitionSpec as P


def extended(block, axis, dim, width):
    count = lax.axis_size(axis)
    forward = [(i, i + 1) for i in range(count - 1)]
    backward = [(target, source) for source, target in forward]
    low = lax.ppermute(
        lax.slice_in_dim(block, block.shape[dim] - width, None, axis=dim), axis, forward
    )
    high = lax.ppermute(lax.slice_in_dim(block, 0, width, axis=dim), axis, backward)
    return jnp.concatenate([low, block, high], axis=dim)


def pair_weights(weight):
    channels = weight.shape[3]
    zeroed = jnp.zeros(weight.shape[:2] + (channels, channels), weight.dtype)
    row_blocks = []
    for time_step in range(3):
        for in_phase in range(2):
            column_blocks = []
            for out_phase in range(2):
                tap_time = 2 * time_step + in_phase - out_phase
                if 0 <= tap_time <= 4:
                    column_blocks.append(weight[:, :, tap_time])
                else:
                    column_blocks.append(zeroed)
            row_blocks.append(jnp.concatenate(column_blocks, axis=3))
    stacked = jnp.concatenate(row_blocks, axis=2)
    return stacked.reshape((-1,) + stacked.shape[2:])


def stack_time(block, dilation):
    pairs = block.shape[2]
    padded = jnp.pad(block, ((0, 0), (2 * dilation, 2 * dilation), (1, 1), (0, 0)))
    stacked = jnp.concatenate(
        [padded[:, :, 0:pairs], padded[:, :, 1 : pairs + 1], padded[:, :, 2 : pairs + 2]],
        axis=3,
    )
    return stacked.reshape(stacked.shape[0], -1, stacked.shape[3])


def spread_call(xs, weights, flat, counts, dilation, pairs):
    shots, rows, lanes = flat.shape
    scalars = jnp.concatenate([jnp.zeros((1,), jnp.int32), counts])
    flops = 2 * shots * 15 * xs.shape[1] * xs.shape[2] * weights.shape[2]
    return pl.pallas_call(
        functools.partial(spread_kernel, dilation=dilation, pairs=pairs),
        grid_spec=pltpu.PrefetchScalarGridSpec(
            num_scalar_prefetch=1,
            grid=(shots,),
            in_specs=[
                pl.BlockSpec(xs.shape, lambda s, c: (0, 0, 0)),
                pl.BlockSpec(weights.shape, lambda s, c: (0, 0, 0)),
                pl.BlockSpec((1, rows, lanes), lambda s, c: (s, 0, 0)),
            ],
            out_specs=pl.BlockSpec((1, rows, lanes), lambda s, c: (s, 0, 0)),
        ),
        out_shape=jax.ShapeDtypeStruct((shots, rows, lanes), jnp.bfloat16),
        compiler_params=pltpu.CompilerParams(vmem_limit_bytes=48 * 1024 * 1024),
        cost_estimate=pl.CostEstimate(
            flops=flops,
            transcendentals=0,
            bytes_accessed=xs.size * 2 + weights.size * 2 + 4 * shots * rows * lanes,
        ),
    )(scalars, xs, weights, flat)


def spread_kernel(scalars_ref, xs_ref, w_ref, res_ref, out_ref, *, dilation, pairs):
    s = pl.program_id(0)
    rows, lanes = out_ref.shape[1:]
    lhs = jnp.concatenate([xs_ref[s + b] for b in range(3)], axis=1)
    rhs = jnp.concatenate(
        [jnp.concatenate([w_ref[a * 3 + b] for a in range(5)], axis=1) for b in range(3)], axis=0
    )
    spread = jnp.dot(lhs, rhs, preferred_element_type=jnp.float32)
    total = None
    for a in range(5):
        part = spread[a * dilation * pairs : a * dilation * pairs + rows, a * lanes : (a + 1) * lanes]
        total = part if total is None else total + part
    first = scalars_ref[0] * (rows // pairs)
    receiver = first + lax.broadcasted_iota(jnp.int32, (rows, lanes), 0) // pairs
    live = receiver < scalars_ref[1 + s]
    value = res_ref[0].astype(jnp.float32) + jnp.maximum(total, 0.0)
    out_ref[0] = jnp.where(live, value, 0.0).astype(out_ref.dtype)


def halos(block, axis):
    count = lax.axis_size(axis)
    forward = [(i, i + 1) for i in range(count - 1)]
    backward = [(target, source) for source, target in forward]
    low = lax.ppermute(block[-1:], axis, forward)
    high = lax.ppermute(block[:1], axis, backward)
    return low, high


def stack_flat(inner, low, high, dilation, pairs):
    volume = jnp.concatenate([low, inner, high], axis=0)
    rows = volume.shape[1]
    phase = (jnp.arange(rows, dtype=jnp.int32) % pairs)[None, :, None]
    blank = jnp.zeros_like(volume[:, :1])
    before = jnp.concatenate([blank, volume[:, :-1]], axis=1)
    after = jnp.concatenate([volume[:, 1:], blank], axis=1)
    before = jnp.where(phase == 0, jnp.zeros_like(before), before)
    after = jnp.where(phase == pairs - 1, jnp.zeros_like(after), after)
    stacked = jnp.concatenate([before, volume, after], axis=2)
    margin = 2 * dilation * pairs
    return jnp.pad(stacked, ((0, 0), (margin, margin), (0, 0)))


def conv_kernel(scalars_ref, xs_ref, w_ref, res_ref, out_ref, acc_ref, *, dilation, pairs):
    s = pl.program_id(0)
    rows = acc_ref.shape[0]
    for a in range(5):
        for b in range(3):
            lhs = xs_ref[s + b, pl.ds(a * dilation * pairs, rows), :]
            contrib = jnp.dot(lhs, w_ref[a * 3 + b], preferred_element_type=jnp.float32)
            if a == 0 and b == 0:
                acc_ref[...] = contrib
            else:
                acc_ref[...] += contrib
    first = scalars_ref[0] * (rows // pairs)
    receiver = first + lax.broadcasted_iota(jnp.int32, acc_ref.shape, 0) // pairs
    live = receiver < scalars_ref[1 + s]
    value = res_ref[0].astype(jnp.float32) + jnp.maximum(acc_ref[...], 0.0)
    out_ref[0] = jnp.where(live, value, 0.0).astype(out_ref.dtype)


def conv_call(xs, weights, flat, counts, dilation, pairs, block, block_rows):
    shots, _, lanes = flat.shape
    window = block_rows + 4 * dilation * pairs
    scalars = jnp.concatenate([jnp.reshape(block, (1,)).astype(jnp.int32), counts])
    flops = 2 * shots * 15 * block_rows * xs.shape[2] * lanes
    return pl.pallas_call(
        functools.partial(conv_kernel, dilation=dilation, pairs=pairs),
        grid_spec=pltpu.PrefetchScalarGridSpec(
            num_scalar_prefetch=1,
            grid=(shots,),
            in_specs=[
                pl.BlockSpec(
                    (pl.Element(xs.shape[0]), pl.Element(window), pl.Element(xs.shape[2])),
                    lambda s, c: (0, c[0] * block_rows, 0),
                ),
                pl.BlockSpec(weights.shape, lambda s, c: (0, 0, 0)),
                pl.BlockSpec((1, block_rows, lanes), lambda s, c: (s, c[0], 0)),
            ],
            out_specs=pl.BlockSpec((1, block_rows, lanes), lambda s, c: (s, 0, 0)),
            scratch_shapes=[pltpu.VMEM((block_rows, lanes), jnp.float32)],
        ),
        out_shape=jax.ShapeDtypeStruct((shots, block_rows, lanes), jnp.bfloat16),
        compiler_params=pltpu.CompilerParams(vmem_limit_bytes=48 * 1024 * 1024),
        cost_estimate=pl.CostEstimate(
            flops=flops,
            transcendentals=0,
            bytes_accessed=xs.shape[0] * window * xs.shape[2] * 2 + weights.size * 2
            + 4 * shots * block_rows * lanes,
        ),
    )(scalars, xs, weights, flat)


def body(features, counts, first_weight, second_weight):
    receivers = features.shape[1]
    shot_local = features.shape[2]
    pairs = features.shape[3]
    lanes = features.shape[4]
    count = lax.axis_size("shot")
    me = lax.axis_index("shot")
    chosen = lax.dynamic_slice_in_dim(counts[:, 0], me * shot_local, shot_local)
    first_pairs = pair_weights(first_weight)
    second_pairs = pair_weights(second_weight)
    volume = jnp.transpose(features[0], (1, 0, 2, 3))
    alive = jnp.arange(receivers, dtype=jnp.int32)[None, :] < chosen[:, None]
    inputs = volume * alive.astype(volume.dtype)[:, :, None, None]
    flat1 = inputs.reshape(shot_local, receivers * pairs, lanes)
    low1, high1 = halos(flat1, "shot")
    xs1 = stack_flat(flat1, low1, high1, 1, pairs)
    flat2 = spread_call(xs1, first_pairs, flat1, chosen, 1, pairs)
    low2, high2 = halos(flat2, "shot")
    xs2 = stack_flat(flat2, low2, high2, 4, pairs)
    span = receivers // count
    whole = spread_call(xs2, second_pairs, flat2, chosen, 4, pairs)
    arrived = []
    for shift in range(count):
        target = lax.rem(me + shift, count)
        piece = lax.dynamic_slice_in_dim(whole, target * span * pairs, span * pairs, axis=1)
        if shift:
            pairs_list = [(i, (i + shift) % count) for i in range(count)]
            piece = lax.ppermute(piece, "shot", pairs_list)
        arrived.append((shift, piece))
    by_shift = jnp.stack([piece for _, piece in sorted(arrived, key=lambda t: t[0])])
    order = lax.rem(me - jnp.arange(count, dtype=jnp.int32) + count, count)
    ordered = jnp.take(by_shift, order, axis=0)
    ordered = ordered.reshape(count * shot_local, span, pairs, lanes)
    return jnp.transpose(ordered, (1, 0, 2, 3))[None]


def solution(mesh):
    placed = (P("cable", None, ("grp", "shot"), None, None), P("grp", "cable"), P(), P())
    return jax.shard_map(
        body,
        mesh=mesh,
        in_specs=placed,
        out_specs=P("cable", "shot", "grp", None, None),
        check_vma=False,
    )
```

```python
import functools

import jax
import jax.numpy as jnp
from jax import lax
from jax.experimental import pallas as pl
from jax.experimental.pallas import tpu as pltpu
from jax.sharding import PartitionSpec as P


def extended(block, axis, dim, width):
    count = lax.axis_size(axis)
    forward = [(i, i + 1) for i in range(count - 1)]
    backward = [(target, source) for source, target in forward]
    low = lax.ppermute(
        lax.slice_in_dim(block, block.shape[dim] - width, None, axis=dim), axis, forward
    )
    high = lax.ppermute(lax.slice_in_dim(block, 0, width, axis=dim), axis, backward)
    return jnp.concatenate([low, block, high], axis=dim)


def pair_weights(weight):
    channels = weight.shape[3]
    zeroed = jnp.zeros(weight.shape[:2] + (channels, channels), weight.dtype)
    row_blocks = []
    for time_step in range(3):
        for in_phase in range(2):
            column_blocks = []
            for out_phase in range(2):
                tap_time = 2 * time_step + in_phase - out_phase
                if 0 <= tap_time <= 4:
                    column_blocks.append(weight[:, :, tap_time])
                else:
                    column_blocks.append(zeroed)
            row_blocks.append(jnp.concatenate(column_blocks, axis=3))
    stacked = jnp.concatenate(row_blocks, axis=2)
    return stacked.reshape((-1,) + stacked.shape[2:])


def stack_time(block, dilation):
    pairs = block.shape[2]
    padded = jnp.pad(block, ((0, 0), (2 * dilation, 2 * dilation), (1, 1), (0, 0)))
    stacked = jnp.concatenate(
        [padded[:, :, 0:pairs], padded[:, :, 1 : pairs + 1], padded[:, :, 2 : pairs + 2]],
        axis=3,
    )
    return stacked.reshape(stacked.shape[0], -1, stacked.shape[3])


def spread_call(xs, weights, flat, counts, dilation, pairs):
    shots, rows, lanes = flat.shape
    scalars = jnp.concatenate([jnp.zeros((1,), jnp.int32), counts])
    flops = 2 * shots * 15 * xs.shape[1] * xs.shape[2] * weights.shape[2]
    return pl.pallas_call(
        functools.partial(spread_kernel, dilation=dilation, pairs=pairs),
        grid_spec=pltpu.PrefetchScalarGridSpec(
            num_scalar_prefetch=1,
            grid=(shots,),
            in_specs=[
                pl.BlockSpec((1, xs.shape[1], xs.shape[2]), lambda s, c: (s, 0, 0)),
                pl.BlockSpec((1, xs.shape[1], xs.shape[2]), lambda s, c: (s + 1, 0, 0)),
                pl.BlockSpec((1, xs.shape[1], xs.shape[2]), lambda s, c: (s + 2, 0, 0)),
                pl.BlockSpec(weights.shape, lambda s, c: (0, 0, 0)),
                pl.BlockSpec((1, rows, lanes), lambda s, c: (s, 0, 0)),
            ],
            out_specs=pl.BlockSpec((1, rows, lanes), lambda s, c: (s, 0, 0)),
        ),
        out_shape=jax.ShapeDtypeStruct((shots, rows, lanes), jnp.bfloat16),
        compiler_params=pltpu.CompilerParams(vmem_limit_bytes=48 * 1024 * 1024),
        cost_estimate=pl.CostEstimate(
            flops=flops,
            transcendentals=0,
            bytes_accessed=xs.size * 2 + weights.size * 2 + 4 * shots * rows * lanes,
        ),
    )(scalars, xs, xs, xs, weights, flat)


def spread_kernel(scalars_ref, x0_ref, x1_ref, x2_ref, w_ref, res_ref, out_ref, *, dilation, pairs):
    s = pl.program_id(0)
    rows, lanes = out_ref.shape[1:]
    lhs = jnp.concatenate([x0_ref[0], x1_ref[0], x2_ref[0]], axis=1)
    rhs = jnp.concatenate(
        [jnp.concatenate([w_ref[a * 3 + b] for a in range(5)], axis=1) for b in range(3)], axis=0
    )
    spread = jnp.dot(lhs, rhs, preferred_element_type=jnp.float32)
    total = None
    for a in range(5):
        part = spread[a * dilation * pairs : a * dilation * pairs + rows, a * lanes : (a + 1) * lanes]
        total = part if total is None else total + part
    first = scalars_ref[0] * (rows // pairs)
    receiver = first + lax.broadcasted_iota(jnp.int32, (rows, lanes), 0) // pairs
    live = receiver < scalars_ref[1 + s]
    value = res_ref[0].astype(jnp.float32) + jnp.maximum(total, 0.0)
    out_ref[0] = jnp.where(live, value, 0.0).astype(out_ref.dtype)


def halos(block, axis):
    count = lax.axis_size(axis)
    forward = [(i, i + 1) for i in range(count - 1)]
    backward = [(target, source) for source, target in forward]
    low = lax.ppermute(block[-1:], axis, forward)
    high = lax.ppermute(block[:1], axis, backward)
    return low, high


def stack_flat(inner, low, high, dilation, pairs):
    volume = jnp.concatenate([low, inner, high], axis=0)
    rows = volume.shape[1]
    phase = (jnp.arange(rows, dtype=jnp.int32) % pairs)[None, :, None]
    blank = jnp.zeros_like(volume[:, :1])
    before = jnp.concatenate([blank, volume[:, :-1]], axis=1)
    after = jnp.concatenate([volume[:, 1:], blank], axis=1)
    before = jnp.where(phase == 0, jnp.zeros_like(before), before)
    after = jnp.where(phase == pairs - 1, jnp.zeros_like(after), after)
    stacked = jnp.concatenate([before, volume, after], axis=2)
    margin = 2 * dilation * pairs
    return jnp.pad(stacked, ((0, 0), (margin, margin), (0, 0)))


def conv_kernel(scalars_ref, xs_ref, w_ref, res_ref, out_ref, acc_ref, *, dilation, pairs):
    s = pl.program_id(0)
    rows = acc_ref.shape[0]
    for a in range(5):
        for b in range(3):
            lhs = xs_ref[s + b, pl.ds(a * dilation * pairs, rows), :]
            contrib = jnp.dot(lhs, w_ref[a * 3 + b], preferred_element_type=jnp.float32)
            if a == 0 and b == 0:
                acc_ref[...] = contrib
            else:
                acc_ref[...] += contrib
    first = scalars_ref[0] * (rows // pairs)
    receiver = first + lax.broadcasted_iota(jnp.int32, acc_ref.shape, 0) // pairs
    live = receiver < scalars_ref[1 + s]
    value = res_ref[0].astype(jnp.float32) + jnp.maximum(acc_ref[...], 0.0)
    out_ref[0] = jnp.where(live, value, 0.0).astype(out_ref.dtype)


def conv_call(xs, weights, flat, counts, dilation, pairs, block, block_rows):
    shots, _, lanes = flat.shape
    window = block_rows + 4 * dilation * pairs
    scalars = jnp.concatenate([jnp.reshape(block, (1,)).astype(jnp.int32), counts])
    flops = 2 * shots * 15 * block_rows * xs.shape[2] * lanes
    return pl.pallas_call(
        functools.partial(conv_kernel, dilation=dilation, pairs=pairs),
        grid_spec=pltpu.PrefetchScalarGridSpec(
            num_scalar_prefetch=1,
            grid=(shots,),
            in_specs=[
                pl.BlockSpec(
                    (pl.Element(xs.shape[0]), pl.Element(window), pl.Element(xs.shape[2])),
                    lambda s, c: (0, c[0] * block_rows, 0),
                ),
                pl.BlockSpec(weights.shape, lambda s, c: (0, 0, 0)),
                pl.BlockSpec((1, block_rows, lanes), lambda s, c: (s, c[0], 0)),
            ],
            out_specs=pl.BlockSpec((1, block_rows, lanes), lambda s, c: (s, 0, 0)),
            scratch_shapes=[pltpu.VMEM((block_rows, lanes), jnp.float32)],
        ),
        out_shape=jax.ShapeDtypeStruct((shots, block_rows, lanes), jnp.bfloat16),
        compiler_params=pltpu.CompilerParams(vmem_limit_bytes=48 * 1024 * 1024),
        cost_estimate=pl.CostEstimate(
            flops=flops,
            transcendentals=0,
            bytes_accessed=xs.shape[0] * window * xs.shape[2] * 2 + weights.size * 2
            + 4 * shots * block_rows * lanes,
        ),
    )(scalars, xs, weights, flat)


def body(features, counts, first_weight, second_weight):
    receivers = features.shape[1]
    shot_local = features.shape[2]
    pairs = features.shape[3]
    lanes = features.shape[4]
    count = lax.axis_size("shot")
    me = lax.axis_index("shot")
    chosen = lax.dynamic_slice_in_dim(counts[:, 0], me * shot_local, shot_local)
    first_pairs = pair_weights(first_weight)
    second_pairs = pair_weights(second_weight)
    volume = jnp.transpose(features[0], (1, 0, 2, 3))
    alive = jnp.arange(receivers, dtype=jnp.int32)[None, :] < chosen[:, None]
    inputs = volume * alive.astype(volume.dtype)[:, :, None, None]
    flat1 = inputs.reshape(shot_local, receivers * pairs, lanes)
    low1, high1 = halos(flat1, "shot")
    xs1 = stack_flat(flat1, low1, high1, 1, pairs)
    flat2 = spread_call(xs1, first_pairs, flat1, chosen, 1, pairs)
    low2, high2 = halos(flat2, "shot")
    xs2 = stack_flat(flat2, low2, high2, 4, pairs)
    span = receivers // count
    whole = spread_call(xs2, second_pairs, flat2, chosen, 4, pairs)
    arrived = []
    for shift in range(count):
        target = lax.rem(me + shift, count)
        piece = lax.dynamic_slice_in_dim(whole, target * span * pairs, span * pairs, axis=1)
        if shift:
            pairs_list = [(i, (i + shift) % count) for i in range(count)]
            piece = lax.ppermute(piece, "shot", pairs_list)
        arrived.append((shift, piece))
    by_shift = [piece for _, piece in sorted(arrived, key=lambda t: t[0])]
    ordered = jnp.concatenate(
        [lax.select_n(lax.rem(me - q + count, count), *by_shift) for q in range(count)], axis=0
    )
    ordered = ordered.reshape(count * shot_local, span, pairs, lanes)
    return jnp.transpose(ordered, (1, 0, 2, 3))[None]


def solution(mesh):
    placed = (P("cable", None, ("grp", "shot"), None, None), P("grp", "cable"), P(), P())
    return jax.shard_map(
        body,
        mesh=mesh,
        in_specs=placed,
        out_specs=P("cable", "shot", "grp", None, None),
        check_vma=False,
    )
```

```python
import functools

import jax
import jax.numpy as jnp
from jax import lax
from jax.experimental import pallas as pl
from jax.experimental.pallas import tpu as pltpu
from jax.sharding import PartitionSpec as P


def extended(block, axis, dim, width):
    count = lax.axis_size(axis)
    forward = [(i, i + 1) for i in range(count - 1)]
    backward = [(target, source) for source, target in forward]
    low = lax.ppermute(
        lax.slice_in_dim(block, block.shape[dim] - width, None, axis=dim), axis, forward
    )
    high = lax.ppermute(lax.slice_in_dim(block, 0, width, axis=dim), axis, backward)
    return jnp.concatenate([low, block, high], axis=dim)


def pair_weights(weight):
    channels = weight.shape[3]
    zeroed = jnp.zeros(weight.shape[:2] + (channels, channels), weight.dtype)
    row_blocks = []
    for time_step in range(3):
        for in_phase in range(2):
            column_blocks = []
            for out_phase in range(2):
                tap_time = 2 * time_step + in_phase - out_phase
                if 0 <= tap_time <= 4:
                    column_blocks.append(weight[:, :, tap_time])
                else:
                    column_blocks.append(zeroed)
            row_blocks.append(jnp.concatenate(column_blocks, axis=3))
    stacked = jnp.concatenate(row_blocks, axis=2)
    return stacked.reshape((-1,) + stacked.shape[2:])


def stack_time(block, dilation):
    pairs = block.shape[2]
    padded = jnp.pad(block, ((0, 0), (2 * dilation, 2 * dilation), (1, 1), (0, 0)))
    stacked = jnp.concatenate(
        [padded[:, :, 0:pairs], padded[:, :, 1 : pairs + 1], padded[:, :, 2 : pairs + 2]],
        axis=3,
    )
    return stacked.reshape(stacked.shape[0], -1, stacked.shape[3])


def spread_call(low, xs, high, weights, flat, counts, dilation, pairs):
    shots, rows, lanes = flat.shape
    scalars = jnp.concatenate([jnp.zeros((1,), jnp.int32), counts])
    flops = 2 * shots * 15 * xs.shape[1] * xs.shape[2] * weights.shape[2]
    return pl.pallas_call(
        functools.partial(spread_kernel, dilation=dilation, pairs=pairs),
        grid_spec=pltpu.PrefetchScalarGridSpec(
            num_scalar_prefetch=1,
            grid=(shots,),
            in_specs=[
                pl.BlockSpec((1, xs.shape[1], xs.shape[2]), lambda s, c: (0, 0, 0)),
                pl.BlockSpec((1, xs.shape[1], xs.shape[2]), lambda s, c: (jnp.maximum(s - 1, 0), 0, 0)),
                pl.BlockSpec((1, xs.shape[1], xs.shape[2]), lambda s, c: (s, 0, 0)),
                pl.BlockSpec(
                    (1, xs.shape[1], xs.shape[2]), lambda s, c: (jnp.minimum(s + 1, shots - 1), 0, 0)
                ),
                pl.BlockSpec((1, xs.shape[1], xs.shape[2]), lambda s, c: (0, 0, 0)),
                pl.BlockSpec(weights.shape, lambda s, c: (0, 0, 0)),
                pl.BlockSpec((1, rows, lanes), lambda s, c: (s, 0, 0)),
            ],
            out_specs=pl.BlockSpec((1, rows, lanes), lambda s, c: (s, 0, 0)),
        ),
        out_shape=jax.ShapeDtypeStruct((shots, rows, lanes), jnp.bfloat16),
        compiler_params=pltpu.CompilerParams(vmem_limit_bytes=48 * 1024 * 1024),
        cost_estimate=pl.CostEstimate(
            flops=flops,
            transcendentals=0,
            bytes_accessed=(xs.size + low.size + high.size) * 2 + weights.size * 2 + 4 * shots * rows * lanes,
        ),
    )(scalars, low, xs, xs, xs, high, weights, flat)


def spread_kernel(scalars_ref, lo_ref, x0_ref, x1_ref, x2_ref, hi_ref, w_ref, res_ref, out_ref, *, dilation, pairs):
    s = pl.program_id(0)
    rows, lanes = out_ref.shape[1:]
    first_shot = jnp.where(s == 0, lo_ref[0], x0_ref[0])
    last_shot = jnp.where(s == pl.num_programs(0) - 1, hi_ref[0], x2_ref[0])
    lhs = jnp.concatenate([first_shot, x1_ref[0], last_shot], axis=1)
    rhs = jnp.concatenate(
        [jnp.concatenate([w_ref[a * 3 + b] for a in range(5)], axis=1) for b in range(3)], axis=0
    )
    spread = jnp.dot(lhs, rhs, preferred_element_type=jnp.float32)
    total = None
    for a in range(5):
        part = spread[a * dilation * pairs : a * dilation * pairs + rows, a * lanes : (a + 1) * lanes]
        total = part if total is None else total + part
    first = scalars_ref[0] * (rows // pairs)
    receiver = first + lax.broadcasted_iota(jnp.int32, (rows, lanes), 0) // pairs
    live = receiver < scalars_ref[1 + s]
    value = res_ref[0].astype(jnp.float32) + jnp.maximum(total, 0.0)
    out_ref[0] = jnp.where(live, value, 0.0).astype(out_ref.dtype)


def halos(block, axis):
    count = lax.axis_size(axis)
    forward = [(i, i + 1) for i in range(count - 1)]
    backward = [(target, source) for source, target in forward]
    low = lax.ppermute(block[-1:], axis, forward)
    high = lax.ppermute(block[:1], axis, backward)
    return low, high


def stack_rows(volume, dilation, pairs):
    rows = volume.shape[1]
    phase = (jnp.arange(rows, dtype=jnp.int32) % pairs)[None, :, None]
    blank = jnp.zeros_like(volume[:, :1])
    before = jnp.concatenate([blank, volume[:, :-1]], axis=1)
    after = jnp.concatenate([volume[:, 1:], blank], axis=1)
    before = jnp.where(phase == 0, jnp.zeros_like(before), before)
    after = jnp.where(phase == pairs - 1, jnp.zeros_like(after), after)
    stacked = jnp.concatenate([before, volume, after], axis=2)
    margin = 2 * dilation * pairs
    return jnp.pad(stacked, ((0, 0), (margin, margin), (0, 0)))


def conv_kernel(scalars_ref, xs_ref, w_ref, res_ref, out_ref, acc_ref, *, dilation, pairs):
    s = pl.program_id(0)
    rows = acc_ref.shape[0]
    for a in range(5):
        for b in range(3):
            lhs = xs_ref[s + b, pl.ds(a * dilation * pairs, rows), :]
            contrib = jnp.dot(lhs, w_ref[a * 3 + b], preferred_element_type=jnp.float32)
            if a == 0 and b == 0:
                acc_ref[...] = contrib
            else:
                acc_ref[...] += contrib
    first = scalars_ref[0] * (rows // pairs)
    receiver = first + lax.broadcasted_iota(jnp.int32, acc_ref.shape, 0) // pairs
    live = receiver < scalars_ref[1 + s]
    value = res_ref[0].astype(jnp.float32) + jnp.maximum(acc_ref[...], 0.0)
    out_ref[0] = jnp.where(live, value, 0.0).astype(out_ref.dtype)


def conv_call(xs, weights, flat, counts, dilation, pairs, block, block_rows):
    shots, _, lanes = flat.shape
    window = block_rows + 4 * dilation * pairs
    scalars = jnp.concatenate([jnp.reshape(block, (1,)).astype(jnp.int32), counts])
    flops = 2 * shots * 15 * block_rows * xs.shape[2] * lanes
    return pl.pallas_call(
        functools.partial(conv_kernel, dilation=dilation, pairs=pairs),
        grid_spec=pltpu.PrefetchScalarGridSpec(
            num_scalar_prefetch=1,
            grid=(shots,),
            in_specs=[
                pl.BlockSpec(
                    (pl.Element(xs.shape[0]), pl.Element(window), pl.Element(xs.shape[2])),
                    lambda s, c: (0, c[0] * block_rows, 0),
                ),
                pl.BlockSpec(weights.shape, lambda s, c: (0, 0, 0)),
                pl.BlockSpec((1, block_rows, lanes), lambda s, c: (s, c[0], 0)),
            ],
            out_specs=pl.BlockSpec((1, block_rows, lanes), lambda s, c: (s, 0, 0)),
            scratch_shapes=[pltpu.VMEM((block_rows, lanes), jnp.float32)],
        ),
        out_shape=jax.ShapeDtypeStruct((shots, block_rows, lanes), jnp.bfloat16),
        compiler_params=pltpu.CompilerParams(vmem_limit_bytes=48 * 1024 * 1024),
        cost_estimate=pl.CostEstimate(
            flops=flops,
            transcendentals=0,
            bytes_accessed=xs.shape[0] * window * xs.shape[2] * 2 + weights.size * 2
            + 4 * shots * block_rows * lanes,
        ),
    )(scalars, xs, weights, flat)


def body(features, counts, first_weight, second_weight):
    receivers = features.shape[1]
    shot_local = features.shape[2]
    pairs = features.shape[3]
    lanes = features.shape[4]
    count = lax.axis_size("shot")
    me = lax.axis_index("shot")
    chosen = lax.dynamic_slice_in_dim(counts[:, 0], me * shot_local, shot_local)
    first_pairs = pair_weights(first_weight)
    second_pairs = pair_weights(second_weight)
    volume = jnp.transpose(features[0], (1, 0, 2, 3)).reshape(shot_local, receivers * pairs, lanes)
    alive = jnp.arange(receivers * pairs, dtype=jnp.int32)[None, :] // pairs < chosen[:, None]
    flat1 = volume * alive.astype(volume.dtype)[:, :, None]
    low1, high1 = halos(flat1, "shot")
    xs1 = stack_rows(flat1, 1, pairs)
    flat2 = spread_call(
        stack_rows(low1, 1, pairs), xs1, stack_rows(high1, 1, pairs), first_pairs, flat1, chosen, 1, pairs
    )
    low2, high2 = halos(flat2, "shot")
    xs2 = stack_rows(flat2, 4, pairs)
    span = receivers // count
    whole = spread_call(
        stack_rows(low2, 4, pairs), xs2, stack_rows(high2, 4, pairs), second_pairs, flat2, chosen, 4, pairs
    )
    arrived = []
    for shift in range(count):
        target = lax.rem(me + shift, count)
        piece = lax.dynamic_slice_in_dim(whole, target * span * pairs, span * pairs, axis=1)
        if shift:
            pairs_list = [(i, (i + shift) % count) for i in range(count)]
            piece = lax.ppermute(piece, "shot", pairs_list)
        arrived.append((shift, piece))
    by_shift = [piece for _, piece in sorted(arrived, key=lambda t: t[0])]
    ordered = jnp.concatenate(
        [lax.select_n(lax.rem(me - q + count, count), *by_shift) for q in range(count)], axis=0
    )
    ordered = ordered.reshape(count * shot_local, span, pairs, lanes)
    return jnp.transpose(ordered, (1, 0, 2, 3))[None]


def solution(mesh):
    placed = (P("cable", None, ("grp", "shot"), None, None), P("grp", "cable"), P(), P())
    return jax.shard_map(
        body,
        mesh=mesh,
        in_specs=placed,
        out_specs=P("cable", "shot", "grp", None, None),
        check_vma=False,
    )
```

```python
import functools

import jax
import jax.numpy as jnp
from jax import lax
from jax.experimental import pallas as pl
from jax.experimental.pallas import tpu as pltpu
from jax.sharding import PartitionSpec as P


def extended(block, axis, dim, width):
    count = lax.axis_size(axis)
    forward = [(i, i + 1) for i in range(count - 1)]
    backward = [(target, source) for source, target in forward]
    low = lax.ppermute(
        lax.slice_in_dim(block, block.shape[dim] - width, None, axis=dim), axis, forward
    )
    high = lax.ppermute(lax.slice_in_dim(block, 0, width, axis=dim), axis, backward)
    return jnp.concatenate([low, block, high], axis=dim)


def pair_weights(weight):
    channels = weight.shape[3]
    zeroed = jnp.zeros(weight.shape[:2] + (channels, channels), weight.dtype)
    row_blocks = []
    for time_step in range(3):
        for in_phase in range(2):
            column_blocks = []
            for out_phase in range(2):
                tap_time = 2 * time_step + in_phase - out_phase
                if 0 <= tap_time <= 4:
                    column_blocks.append(weight[:, :, tap_time])
                else:
                    column_blocks.append(zeroed)
            row_blocks.append(jnp.concatenate(column_blocks, axis=3))
    stacked = jnp.concatenate(row_blocks, axis=2)
    return stacked.reshape((-1,) + stacked.shape[2:])


def stack_time(block, dilation):
    pairs = block.shape[2]
    padded = jnp.pad(block, ((0, 0), (2 * dilation, 2 * dilation), (1, 1), (0, 0)))
    stacked = jnp.concatenate(
        [padded[:, :, 0:pairs], padded[:, :, 1 : pairs + 1], padded[:, :, 2 : pairs + 2]],
        axis=3,
    )
    return stacked.reshape(stacked.shape[0], -1, stacked.shape[3])


def spread_call(low, xs, high, weights, flat, counts, dilation, pairs):
    shots, rows, lanes = flat.shape
    scalars = jnp.concatenate([jnp.zeros((1,), jnp.int32), counts])
    flops = 2 * shots * 15 * xs.shape[1] * xs.shape[2] * weights.shape[2]
    return pl.pallas_call(
        functools.partial(spread_kernel, dilation=dilation, pairs=pairs),
        grid_spec=pltpu.PrefetchScalarGridSpec(
            num_scalar_prefetch=1,
            grid=(shots,),
            in_specs=[
                pl.BlockSpec((1, xs.shape[1], xs.shape[2]), lambda s, c: (0, 0, 0)),
                pl.BlockSpec((1, xs.shape[1], xs.shape[2]), lambda s, c: (jnp.maximum(s - 1, 0), 0, 0)),
                pl.BlockSpec((1, xs.shape[1], xs.shape[2]), lambda s, c: (s, 0, 0)),
                pl.BlockSpec(
                    (1, xs.shape[1], xs.shape[2]), lambda s, c: (jnp.minimum(s + 1, shots - 1), 0, 0)
                ),
                pl.BlockSpec((1, xs.shape[1], xs.shape[2]), lambda s, c: (0, 0, 0)),
                pl.BlockSpec(weights.shape, lambda s, c: (0, 0, 0)),
                pl.BlockSpec((1, rows, lanes), lambda s, c: (s, 0, 0)),
            ],
            out_specs=pl.BlockSpec((1, rows, lanes), lambda s, c: (s, 0, 0)),
        ),
        out_shape=jax.ShapeDtypeStruct((shots, rows, lanes), jnp.bfloat16),
        compiler_params=pltpu.CompilerParams(vmem_limit_bytes=48 * 1024 * 1024),
        cost_estimate=pl.CostEstimate(
            flops=flops,
            transcendentals=0,
            bytes_accessed=(xs.size + low.size + high.size) * 2 + weights.size * 2 + 4 * shots * rows * lanes,
        ),
    )(scalars, low, xs, xs, xs, high, weights, flat)


def spread_kernel(scalars_ref, lo_ref, x0_ref, x1_ref, x2_ref, hi_ref, w_ref, res_ref, out_ref, *, dilation, pairs):
    s = pl.program_id(0)
    rows, lanes = out_ref.shape[1:]
    first_shot = jnp.where(s == 0, lo_ref[0], x0_ref[0])
    last_shot = jnp.where(s == pl.num_programs(0) - 1, hi_ref[0], x2_ref[0])
    lhs = jnp.concatenate([first_shot, x1_ref[0], last_shot], axis=1)
    rhs = jnp.concatenate(
        [jnp.concatenate([w_ref[a * 3 + b] for a in range(5)], axis=1) for b in range(3)], axis=0
    )
    spread = jnp.dot(lhs, rhs, preferred_element_type=jnp.float32)
    total = None
    for a in range(5):
        part = spread[a * dilation * pairs : a * dilation * pairs + rows, a * lanes : (a + 1) * lanes]
        total = part if total is None else total + part
    first = scalars_ref[0] * (rows // pairs)
    receiver = first + lax.broadcasted_iota(jnp.int32, (rows, lanes), 0) // pairs
    live = receiver < scalars_ref[1 + s]
    value = res_ref[0].astype(jnp.float32) + jnp.maximum(total, 0.0)
    out_ref[0] = jnp.where(live, value, 0.0).astype(out_ref.dtype)


def halos(block, axis):
    count = lax.axis_size(axis)
    me = lax.axis_index(axis)
    forward = [(i, (i + 1) % count) for i in range(count)]
    backward = [((i + 1) % count, i) for i in range(count)]
    low = lax.ppermute(block[-1:], axis, forward)
    high = lax.ppermute(block[:1], axis, backward)
    low = jnp.where(me == 0, jnp.zeros_like(low), low)
    high = jnp.where(me == count - 1, jnp.zeros_like(high), high)
    return low, high


def stack_rows(volume, dilation, pairs):
    rows = volume.shape[1]
    phase = (jnp.arange(rows, dtype=jnp.int32) % pairs)[None, :, None]
    blank = jnp.zeros_like(volume[:, :1])
    before = jnp.concatenate([blank, volume[:, :-1]], axis=1)
    after = jnp.concatenate([volume[:, 1:], blank], axis=1)
    before = jnp.where(phase == 0, jnp.zeros_like(before), before)
    after = jnp.where(phase == pairs - 1, jnp.zeros_like(after), after)
    stacked = jnp.concatenate([before, volume, after], axis=2)
    margin = 2 * dilation * pairs
    return jnp.pad(stacked, ((0, 0), (margin, margin), (0, 0)))


def conv_kernel(scalars_ref, xs_ref, w_ref, res_ref, out_ref, acc_ref, *, dilation, pairs):
    s = pl.program_id(0)
    rows = acc_ref.shape[0]
    for a in range(5):
        for b in range(3):
            lhs = xs_ref[s + b, pl.ds(a * dilation * pairs, rows), :]
            contrib = jnp.dot(lhs, w_ref[a * 3 + b], preferred_element_type=jnp.float32)
            if a == 0 and b == 0:
                acc_ref[...] = contrib
            else:
                acc_ref[...] += contrib
    first = scalars_ref[0] * (rows // pairs)
    receiver = first + lax.broadcasted_iota(jnp.int32, acc_ref.shape, 0) // pairs
    live = receiver < scalars_ref[1 + s]
    value = res_ref[0].astype(jnp.float32) + jnp.maximum(acc_ref[...], 0.0)
    out_ref[0] = jnp.where(live, value, 0.0).astype(out_ref.dtype)


def conv_call(xs, weights, flat, counts, dilation, pairs, block, block_rows):
    shots, _, lanes = flat.shape
    window = block_rows + 4 * dilation * pairs
    scalars = jnp.concatenate([jnp.reshape(block, (1,)).astype(jnp.int32), counts])
    flops = 2 * shots * 15 * block_rows * xs.shape[2] * lanes
    return pl.pallas_call(
        functools.partial(conv_kernel, dilation=dilation, pairs=pairs),
        grid_spec=pltpu.PrefetchScalarGridSpec(
            num_scalar_prefetch=1,
            grid=(shots,),
            in_specs=[
                pl.BlockSpec(
                    (pl.Element(xs.shape[0]), pl.Element(window), pl.Element(xs.shape[2])),
                    lambda s, c: (0, c[0] * block_rows, 0),
                ),
                pl.BlockSpec(weights.shape, lambda s, c: (0, 0, 0)),
                pl.BlockSpec((1, block_rows, lanes), lambda s, c: (s, c[0], 0)),
            ],
            out_specs=pl.BlockSpec((1, block_rows, lanes), lambda s, c: (s, 0, 0)),
            scratch_shapes=[pltpu.VMEM((block_rows, lanes), jnp.float32)],
        ),
        out_shape=jax.ShapeDtypeStruct((shots, block_rows, lanes), jnp.bfloat16),
        compiler_params=pltpu.CompilerParams(vmem_limit_bytes=48 * 1024 * 1024),
        cost_estimate=pl.CostEstimate(
            flops=flops,
            transcendentals=0,
            bytes_accessed=xs.shape[0] * window * xs.shape[2] * 2 + weights.size * 2
            + 4 * shots * block_rows * lanes,
        ),
    )(scalars, xs, weights, flat)


def body(features, counts, first_weight, second_weight):
    receivers = features.shape[1]
    shot_local = features.shape[2]
    pairs = features.shape[3]
    lanes = features.shape[4]
    count = lax.axis_size("shot")
    me = lax.axis_index("shot")
    chosen = lax.dynamic_slice_in_dim(counts[:, 0], me * shot_local, shot_local)
    first_pairs = pair_weights(first_weight)
    second_pairs = pair_weights(second_weight)
    volume = jnp.transpose(features[0], (1, 0, 2, 3)).reshape(shot_local, receivers * pairs, lanes)
    alive = jnp.arange(receivers * pairs, dtype=jnp.int32)[None, :] // pairs < chosen[:, None]
    flat1 = volume * alive.astype(volume.dtype)[:, :, None]
    low1, high1 = halos(flat1, "shot")
    xs1 = stack_rows(flat1, 1, pairs)
    flat2 = spread_call(
        stack_rows(low1, 1, pairs), xs1, stack_rows(high1, 1, pairs), first_pairs, flat1, chosen, 1, pairs
    )
    low2, high2 = halos(flat2, "shot")
    xs2 = stack_rows(flat2, 4, pairs)
    span = receivers // count
    whole = spread_call(
        stack_rows(low2, 4, pairs), xs2, stack_rows(high2, 4, pairs), second_pairs, flat2, chosen, 4, pairs
    )
    arrived = []
    for shift in range(count):
        target = lax.rem(me + shift, count)
        piece = lax.dynamic_slice_in_dim(whole, target * span * pairs, span * pairs, axis=1)
        if shift:
            pairs_list = [(i, (i + shift) % count) for i in range(count)]
            piece = lax.ppermute(piece, "shot", pairs_list)
        arrived.append((shift, piece))
    by_shift = [piece for _, piece in sorted(arrived, key=lambda t: t[0])]
    ordered = jnp.concatenate(
        [lax.select_n(lax.rem(me - q + count, count), *by_shift) for q in range(count)], axis=0
    )
    ordered = ordered.reshape(count * shot_local, span, pairs, lanes)
    return jnp.transpose(ordered, (1, 0, 2, 3))[None]


def solution(mesh):
    placed = (P("cable", None, ("grp", "shot"), None, None), P("grp", "cable"), P(), P())
    return jax.shard_map(
        body,
        mesh=mesh,
        in_specs=placed,
        out_specs=P("cable", "shot", "grp", None, None),
        check_vma=False,
    )
```

```python
import functools

import jax
import jax.numpy as jnp
from jax import lax
from jax.experimental import pallas as pl
from jax.experimental.pallas import tpu as pltpu
from jax.sharding import PartitionSpec as P


def extended(block, axis, dim, width):
    count = lax.axis_size(axis)
    forward = [(i, i + 1) for i in range(count - 1)]
    backward = [(target, source) for source, target in forward]
    low = lax.ppermute(
        lax.slice_in_dim(block, block.shape[dim] - width, None, axis=dim), axis, forward
    )
    high = lax.ppermute(lax.slice_in_dim(block, 0, width, axis=dim), axis, backward)
    return jnp.concatenate([low, block, high], axis=dim)


def pair_weights(weight):
    ahead = jnp.pad(weight, ((0, 0), (0, 0), (0, 1), (0, 0), (0, 0)))
    behind = jnp.pad(weight, ((0, 0), (0, 0), (1, 0), (0, 0), (0, 0)))
    joined = jnp.concatenate([ahead, behind], axis=4)
    return joined.reshape(weight.shape[0] * weight.shape[1], -1, joined.shape[4])

def stack_time(block, dilation):
    pairs = block.shape[2]
    padded = jnp.pad(block, ((0, 0), (2 * dilation, 2 * dilation), (1, 1), (0, 0)))
    stacked = jnp.concatenate(
        [padded[:, :, 0:pairs], padded[:, :, 1 : pairs + 1], padded[:, :, 2 : pairs + 2]],
        axis=3,
    )
    return stacked.reshape(stacked.shape[0], -1, stacked.shape[3])


def spread_call(low, xs, high, weights, flat, counts, dilation, pairs):
    shots, rows, lanes = flat.shape
    scalars = jnp.concatenate([jnp.zeros((1,), jnp.int32), counts])
    flops = 2 * shots * 15 * xs.shape[1] * xs.shape[2] * weights.shape[2]
    return pl.pallas_call(
        functools.partial(spread_kernel, dilation=dilation, pairs=pairs),
        grid_spec=pltpu.PrefetchScalarGridSpec(
            num_scalar_prefetch=1,
            grid=(shots,),
            in_specs=[
                pl.BlockSpec((1, xs.shape[1], xs.shape[2]), lambda s, c: (0, 0, 0)),
                pl.BlockSpec((1, xs.shape[1], xs.shape[2]), lambda s, c: (jnp.maximum(s - 1, 0), 0, 0)),
                pl.BlockSpec((1, xs.shape[1], xs.shape[2]), lambda s, c: (s, 0, 0)),
                pl.BlockSpec(
                    (1, xs.shape[1], xs.shape[2]), lambda s, c: (jnp.minimum(s + 1, shots - 1), 0, 0)
                ),
                pl.BlockSpec((1, xs.shape[1], xs.shape[2]), lambda s, c: (0, 0, 0)),
                pl.BlockSpec(weights.shape, lambda s, c: (0, 0, 0)),
                pl.BlockSpec((1, rows, lanes), lambda s, c: (s, 0, 0)),
            ],
            out_specs=pl.BlockSpec((1, rows, lanes), lambda s, c: (s, 0, 0)),
        ),
        out_shape=jax.ShapeDtypeStruct((shots, rows, lanes), jnp.bfloat16),
        compiler_params=pltpu.CompilerParams(vmem_limit_bytes=48 * 1024 * 1024),
        cost_estimate=pl.CostEstimate(
            flops=flops,
            transcendentals=0,
            bytes_accessed=(xs.size + low.size + high.size) * 2 + weights.size * 2 + 4 * shots * rows * lanes,
        ),
    )(scalars, low, xs, xs, xs, high, weights, flat)


def spread_kernel(scalars_ref, lo_ref, x0_ref, x1_ref, x2_ref, hi_ref, w_ref, res_ref, out_ref, *, dilation, pairs):
    s = pl.program_id(0)
    rows, lanes = out_ref.shape[1:]
    first_shot = jnp.where(s == 0, lo_ref[0], x0_ref[0])
    last_shot = jnp.where(s == pl.num_programs(0) - 1, hi_ref[0], x2_ref[0])
    lhs = jnp.concatenate([first_shot, x1_ref[0], last_shot], axis=1)
    rhs = jnp.concatenate(
        [jnp.concatenate([w_ref[a * 3 + b] for a in range(5)], axis=1) for b in range(3)], axis=0
    )
    spread = jnp.dot(lhs, rhs, preferred_element_type=jnp.float32)
    total = None
    for a in range(5):
        part = spread[a * dilation * pairs : a * dilation * pairs + rows, a * lanes : (a + 1) * lanes]
        total = part if total is None else total + part
    first = scalars_ref[0] * (rows // pairs)
    receiver = first + lax.broadcasted_iota(jnp.int32, (rows, lanes), 0) // pairs
    live = receiver < scalars_ref[1 + s]
    value = res_ref[0].astype(jnp.float32) + jnp.maximum(total, 0.0)
    out_ref[0] = jnp.where(live, value, 0.0).astype(out_ref.dtype)


def halos(block, axis):
    count = lax.axis_size(axis)
    me = lax.axis_index(axis)
    forward = [(i, (i + 1) % count) for i in range(count)]
    backward = [((i + 1) % count, i) for i in range(count)]
    low = lax.ppermute(block[-1:], axis, forward)
    high = lax.ppermute(block[:1], axis, backward)
    low = jnp.where(me == 0, jnp.zeros_like(low), low)
    high = jnp.where(me == count - 1, jnp.zeros_like(high), high)
    return low, high


def stack_rows(volume, dilation, pairs):
    rows = volume.shape[1]
    phase = (jnp.arange(rows, dtype=jnp.int32) % pairs)[None, :, None]
    blank = jnp.zeros_like(volume[:, :1])
    before = jnp.concatenate([blank, volume[:, :-1]], axis=1)
    after = jnp.concatenate([volume[:, 1:], blank], axis=1)
    before = jnp.where(phase == 0, jnp.zeros_like(before), before)
    after = jnp.where(phase == pairs - 1, jnp.zeros_like(after), after)
    stacked = jnp.concatenate([before, volume, after], axis=2)
    margin = 2 * dilation * pairs
    return jnp.pad(stacked, ((0, 0), (margin, margin), (0, 0)))


def conv_kernel(scalars_ref, xs_ref, w_ref, res_ref, out_ref, acc_ref, *, dilation, pairs):
    s = pl.program_id(0)
    rows = acc_ref.shape[0]
    for a in range(5):
        for b in range(3):
            lhs = xs_ref[s + b, pl.ds(a * dilation * pairs, rows), :]
            contrib = jnp.dot(lhs, w_ref[a * 3 + b], preferred_element_type=jnp.float32)
            if a == 0 and b == 0:
                acc_ref[...] = contrib
            else:
                acc_ref[...] += contrib
    first = scalars_ref[0] * (rows // pairs)
    receiver = first + lax.broadcasted_iota(jnp.int32, acc_ref.shape, 0) // pairs
    live = receiver < scalars_ref[1 + s]
    value = res_ref[0].astype(jnp.float32) + jnp.maximum(acc_ref[...], 0.0)
    out_ref[0] = jnp.where(live, value, 0.0).astype(out_ref.dtype)


def conv_call(xs, weights, flat, counts, dilation, pairs, block, block_rows):
    shots, _, lanes = flat.shape
    window = block_rows + 4 * dilation * pairs
    scalars = jnp.concatenate([jnp.reshape(block, (1,)).astype(jnp.int32), counts])
    flops = 2 * shots * 15 * block_rows * xs.shape[2] * lanes
    return pl.pallas_call(
        functools.partial(conv_kernel, dilation=dilation, pairs=pairs),
        grid_spec=pltpu.PrefetchScalarGridSpec(
            num_scalar_prefetch=1,
            grid=(shots,),
            in_specs=[
                pl.BlockSpec(
                    (pl.Element(xs.shape[0]), pl.Element(window), pl.Element(xs.shape[2])),
                    lambda s, c: (0, c[0] * block_rows, 0),
                ),
                pl.BlockSpec(weights.shape, lambda s, c: (0, 0, 0)),
                pl.BlockSpec((1, block_rows, lanes), lambda s, c: (s, c[0], 0)),
            ],
            out_specs=pl.BlockSpec((1, block_rows, lanes), lambda s, c: (s, 0, 0)),
            scratch_shapes=[pltpu.VMEM((block_rows, lanes), jnp.float32)],
        ),
        out_shape=jax.ShapeDtypeStruct((shots, block_rows, lanes), jnp.bfloat16),
        compiler_params=pltpu.CompilerParams(vmem_limit_bytes=48 * 1024 * 1024),
        cost_estimate=pl.CostEstimate(
            flops=flops,
            transcendentals=0,
            bytes_accessed=xs.shape[0] * window * xs.shape[2] * 2 + weights.size * 2
            + 4 * shots * block_rows * lanes,
        ),
    )(scalars, xs, weights, flat)


def body(features, counts, first_weight, second_weight):
    receivers = features.shape[1]
    shot_local = features.shape[2]
    pairs = features.shape[3]
    lanes = features.shape[4]
    count = lax.axis_size("shot")
    me = lax.axis_index("shot")
    chosen = lax.dynamic_slice_in_dim(counts[:, 0], me * shot_local, shot_local)
    first_pairs = pair_weights(first_weight)
    second_pairs = pair_weights(second_weight)
    volume = jnp.transpose(features[0], (1, 0, 2, 3)).reshape(shot_local, receivers * pairs, lanes)
    alive = jnp.arange(receivers * pairs, dtype=jnp.int32)[None, :] // pairs < chosen[:, None]
    flat1 = volume * alive.astype(volume.dtype)[:, :, None]
    low1, high1 = halos(flat1, "shot")
    xs1 = stack_rows(flat1, 1, pairs)
    flat2 = spread_call(
        stack_rows(low1, 1, pairs), xs1, stack_rows(high1, 1, pairs), first_pairs, flat1, chosen, 1, pairs
    )
    low2, high2 = halos(flat2, "shot")
    xs2 = stack_rows(flat2, 4, pairs)
    span = receivers // count
    whole = spread_call(
        stack_rows(low2, 4, pairs), xs2, stack_rows(high2, 4, pairs), second_pairs, flat2, chosen, 4, pairs
    )
    arrived = []
    for shift in range(count):
        target = lax.rem(me + shift, count)
        piece = lax.dynamic_slice_in_dim(whole, target * span * pairs, span * pairs, axis=1)
        if shift:
            pairs_list = [(i, (i + shift) % count) for i in range(count)]
            piece = lax.ppermute(piece, "shot", pairs_list)
        arrived.append((shift, piece))
    by_shift = [piece for _, piece in sorted(arrived, key=lambda t: t[0])]
    ordered = jnp.concatenate(
        [lax.select_n(lax.rem(me - q + count, count), *by_shift) for q in range(count)], axis=0
    )
    ordered = ordered.reshape(count * shot_local, span, pairs, lanes)
    return jnp.transpose(ordered, (1, 0, 2, 3))[None]


def solution(mesh):
    placed = (P("cable", None, ("grp", "shot"), None, None), P("grp", "cable"), P(), P())
    return jax.shard_map(
        body,
        mesh=mesh,
        in_specs=placed,
        out_specs=P("cable", "shot", "grp", None, None),
        check_vma=False,
    )
```

```python
import functools

import jax
import jax.numpy as jnp
from jax import lax
from jax.experimental import pallas as pl
from jax.experimental.pallas import tpu as pltpu
from jax.sharding import PartitionSpec as P


def extended(block, axis, dim, width):
    count = lax.axis_size(axis)
    forward = [(i, i + 1) for i in range(count - 1)]
    backward = [(target, source) for source, target in forward]
    low = lax.ppermute(
        lax.slice_in_dim(block, block.shape[dim] - width, None, axis=dim), axis, forward
    )
    high = lax.ppermute(lax.slice_in_dim(block, 0, width, axis=dim), axis, backward)
    return jnp.concatenate([low, block, high], axis=dim)


def pair_weights(weight):
    ahead = jnp.pad(weight, ((0, 0), (0, 0), (0, 1), (0, 0), (0, 0)))
    behind = jnp.pad(weight, ((0, 0), (0, 0), (1, 0), (0, 0), (0, 0)))
    joined = jnp.concatenate([ahead, behind], axis=4)
    return joined.reshape(weight.shape[0] * weight.shape[1], -1, joined.shape[4])

def stack_time(block, dilation):
    pairs = block.shape[2]
    padded = jnp.pad(block, ((0, 0), (2 * dilation, 2 * dilation), (1, 1), (0, 0)))
    stacked = jnp.concatenate(
        [padded[:, :, 0:pairs], padded[:, :, 1 : pairs + 1], padded[:, :, 2 : pairs + 2]],
        axis=3,
    )
    return stacked.reshape(stacked.shape[0], -1, stacked.shape[3])


def spread_call(low, xs, high, weights, flat, counts, dilation, pairs):
    shots, rows, lanes = flat.shape
    scalars = jnp.concatenate([jnp.zeros((1,), jnp.int32), counts])
    flops = 2 * shots * 3 * xs.shape[1] * xs.shape[2] * 5 * lanes
    return pl.pallas_call(
        functools.partial(spread_kernel, dilation=dilation, pairs=pairs),
        grid_spec=pltpu.PrefetchScalarGridSpec(
            num_scalar_prefetch=1,
            grid=(shots,),
            in_specs=[
                pl.BlockSpec((1, xs.shape[1], xs.shape[2]), lambda s, c: (0, 0, 0)),
                pl.BlockSpec((1, xs.shape[1], xs.shape[2]), lambda s, c: (jnp.maximum(s - 1, 0), 0, 0)),
                pl.BlockSpec((1, xs.shape[1], xs.shape[2]), lambda s, c: (s, 0, 0)),
                pl.BlockSpec(
                    (1, xs.shape[1], xs.shape[2]), lambda s, c: (jnp.minimum(s + 1, shots - 1), 0, 0)
                ),
                pl.BlockSpec((1, xs.shape[1], xs.shape[2]), lambda s, c: (0, 0, 0)),
                pl.BlockSpec(weights.shape, lambda s, c: (0, 0, 0, 0, 0)),
                pl.BlockSpec((1, rows, lanes), lambda s, c: (s, 0, 0)),
            ],
            out_specs=pl.BlockSpec((1, rows, lanes), lambda s, c: (s, 0, 0)),
            scratch_shapes=[pltpu.VMEM((3 * xs.shape[2], 5 * lanes), weights.dtype)],
        ),
        out_shape=jax.ShapeDtypeStruct((shots, rows, lanes), jnp.bfloat16),
        compiler_params=pltpu.CompilerParams(vmem_limit_bytes=48 * 1024 * 1024),
        cost_estimate=pl.CostEstimate(
            flops=flops,
            transcendentals=0,
            bytes_accessed=(xs.size + low.size + high.size) * 2 + weights.size * 2 + 4 * shots * rows * lanes,
        ),
    )(scalars, low, xs, xs, xs, high, weights, flat)


def spread_kernel(
    scalars_ref, lo_ref, x0_ref, x1_ref, x2_ref, hi_ref, w_ref, res_ref, out_ref, rhs_ref, *, dilation, pairs
):
    s = pl.program_id(0)
    receiver_taps, shot_taps, time_taps, channels, _ = w_ref.shape

    @pl.when(s == 0)
    def _():
        zero = jnp.zeros((channels, channels), rhs_ref.dtype)
        for b in range(shot_taps):
            for e in range(time_taps + 1):
                row = (b * (time_taps + 1) + e) * channels
                for a in range(receiver_taps):
                    ahead = w_ref[a, b, e] if e < time_taps else zero
                    behind = w_ref[a, b, e - 1] if e >= 1 else zero
                    rhs_ref[pl.ds(row, channels), pl.ds(a * 2 * channels, 2 * channels)] = jnp.concatenate(
                        [ahead, behind], axis=1
                    )

    rows, lanes = out_ref.shape[1:]
    first_shot = jnp.where(s == 0, lo_ref[0], x0_ref[0])
    last_shot = jnp.where(s == pl.num_programs(0) - 1, hi_ref[0], x2_ref[0])
    lhs = jnp.concatenate([first_shot, x1_ref[0], last_shot], axis=1)
    spread = jnp.dot(lhs, rhs_ref[...], preferred_element_type=jnp.float32)
    total = None
    for a in range(5):
        part = spread[a * dilation * pairs : a * dilation * pairs + rows, a * lanes : (a + 1) * lanes]
        total = part if total is None else total + part
    first = scalars_ref[0] * (rows // pairs)
    receiver = first + lax.broadcasted_iota(jnp.int32, (rows, lanes), 0) // pairs
    live = receiver < scalars_ref[1 + s]
    value = res_ref[0].astype(jnp.float32) + jnp.maximum(total, 0.0)
    out_ref[0] = jnp.where(live, value, 0.0).astype(out_ref.dtype)


def halos(block, axis):
    count = lax.axis_size(axis)
    me = lax.axis_index(axis)
    forward = [(i, (i + 1) % count) for i in range(count)]
    backward = [((i + 1) % count, i) for i in range(count)]
    low = lax.ppermute(block[-1:], axis, forward)
    high = lax.ppermute(block[:1], axis, backward)
    low = jnp.where(me == 0, jnp.zeros_like(low), low)
    high = jnp.where(me == count - 1, jnp.zeros_like(high), high)
    return low, high


def stack_rows(volume, dilation, pairs):
    rows = volume.shape[1]
    phase = (jnp.arange(rows, dtype=jnp.int32) % pairs)[None, :, None]
    blank = jnp.zeros_like(volume[:, :1])
    before = jnp.concatenate([blank, volume[:, :-1]], axis=1)
    after = jnp.concatenate([volume[:, 1:], blank], axis=1)
    before = jnp.where(phase == 0, jnp.zeros_like(before), before)
    after = jnp.where(phase == pairs - 1, jnp.zeros_like(after), after)
    stacked = jnp.concatenate([before, volume, after], axis=2)
    margin = 2 * dilation * pairs
    return jnp.pad(stacked, ((0, 0), (margin, margin), (0, 0)))


def conv_kernel(scalars_ref, xs_ref, w_ref, res_ref, out_ref, acc_ref, *, dilation, pairs):
    s = pl.program_id(0)
    rows = acc_ref.shape[0]
    for a in range(5):
        for b in range(3):
            lhs = xs_ref[s + b, pl.ds(a * dilation * pairs, rows), :]
            contrib = jnp.dot(lhs, w_ref[a * 3 + b], preferred_element_type=jnp.float32)
            if a == 0 and b == 0:
                acc_ref[...] = contrib
            else:
                acc_ref[...] += contrib
    first = scalars_ref[0] * (rows // pairs)
    receiver = first + lax.broadcasted_iota(jnp.int32, acc_ref.shape, 0) // pairs
    live = receiver < scalars_ref[1 + s]
    value = res_ref[0].astype(jnp.float32) + jnp.maximum(acc_ref[...], 0.0)
    out_ref[0] = jnp.where(live, value, 0.0).astype(out_ref.dtype)


def conv_call(xs, weights, flat, counts, dilation, pairs, block, block_rows):
    shots, _, lanes = flat.shape
    window = block_rows + 4 * dilation * pairs
    scalars = jnp.concatenate([jnp.reshape(block, (1,)).astype(jnp.int32), counts])
    flops = 2 * shots * 15 * block_rows * xs.shape[2] * lanes
    return pl.pallas_call(
        functools.partial(conv_kernel, dilation=dilation, pairs=pairs),
        grid_spec=pltpu.PrefetchScalarGridSpec(
            num_scalar_prefetch=1,
            grid=(shots,),
            in_specs=[
                pl.BlockSpec(
                    (pl.Element(xs.shape[0]), pl.Element(window), pl.Element(xs.shape[2])),
                    lambda s, c: (0, c[0] * block_rows, 0),
                ),
                pl.BlockSpec(weights.shape, lambda s, c: (0, 0, 0)),
                pl.BlockSpec((1, block_rows, lanes), lambda s, c: (s, c[0], 0)),
            ],
            out_specs=pl.BlockSpec((1, block_rows, lanes), lambda s, c: (s, 0, 0)),
            scratch_shapes=[pltpu.VMEM((block_rows, lanes), jnp.float32)],
        ),
        out_shape=jax.ShapeDtypeStruct((shots, block_rows, lanes), jnp.bfloat16),
        compiler_params=pltpu.CompilerParams(vmem_limit_bytes=48 * 1024 * 1024),
        cost_estimate=pl.CostEstimate(
            flops=flops,
            transcendentals=0,
            bytes_accessed=xs.shape[0] * window * xs.shape[2] * 2 + weights.size * 2
            + 4 * shots * block_rows * lanes,
        ),
    )(scalars, xs, weights, flat)


def body(features, counts, first_weight, second_weight):
    receivers = features.shape[1]
    shot_local = features.shape[2]
    pairs = features.shape[3]
    lanes = features.shape[4]
    count = lax.axis_size("shot")
    me = lax.axis_index("shot")
    chosen = lax.dynamic_slice_in_dim(counts[:, 0], me * shot_local, shot_local)
    volume = jnp.transpose(features[0], (1, 0, 2, 3)).reshape(shot_local, receivers * pairs, lanes)
    alive = jnp.arange(receivers * pairs, dtype=jnp.int32)[None, :] // pairs < chosen[:, None]
    flat1 = volume * alive.astype(volume.dtype)[:, :, None]
    low1, high1 = halos(flat1, "shot")
    xs1 = stack_rows(flat1, 1, pairs)
    flat2 = spread_call(
        stack_rows(low1, 1, pairs), xs1, stack_rows(high1, 1, pairs), first_weight, flat1, chosen, 1, pairs
    )
    low2, high2 = halos(flat2, "shot")
    xs2 = stack_rows(flat2, 4, pairs)
    span = receivers // count
    whole = spread_call(
        stack_rows(low2, 4, pairs), xs2, stack_rows(high2, 4, pairs), second_weight, flat2, chosen, 4, pairs
    )
    arrived = []
    for shift in range(count):
        target = lax.rem(me + shift, count)
        piece = lax.dynamic_slice_in_dim(whole, target * span * pairs, span * pairs, axis=1)
        if shift:
            pairs_list = [(i, (i + shift) % count) for i in range(count)]
            piece = lax.ppermute(piece, "shot", pairs_list)
        arrived.append((shift, piece))
    by_shift = [piece for _, piece in sorted(arrived, key=lambda t: t[0])]
    ordered = jnp.concatenate(
        [lax.select_n(lax.rem(me - q + count, count), *by_shift) for q in range(count)], axis=0
    )
    ordered = ordered.reshape(count * shot_local, span, pairs, lanes)
    return jnp.transpose(ordered, (1, 0, 2, 3))[None]


def solution(mesh):
    placed = (P("cable", None, ("grp", "shot"), None, None), P("grp", "cable"), P(), P())
    return jax.shard_map(
        body,
        mesh=mesh,
        in_specs=placed,
        out_specs=P("cable", "shot", "grp", None, None),
        check_vma=False,
    )
```

```python
import functools

import jax
import jax.numpy as jnp
from jax import lax
from jax.experimental import pallas as pl
from jax.experimental.pallas import tpu as pltpu
from jax.sharding import PartitionSpec as P


def spread_call(low, xs, high, weights, flat, counts, dilation, pairs):
    shots, rows, lanes = flat.shape
    scalars = jnp.concatenate([jnp.zeros((1,), jnp.int32), counts])
    flops = 2 * shots * 3 * xs.shape[1] * xs.shape[2] * 5 * lanes
    return pl.pallas_call(
        functools.partial(spread_kernel, dilation=dilation, pairs=pairs),
        grid_spec=pltpu.PrefetchScalarGridSpec(
            num_scalar_prefetch=1,
            grid=(shots,),
            in_specs=[
                pl.BlockSpec((1, xs.shape[1], xs.shape[2]), lambda s, c: (0, 0, 0)),
                pl.BlockSpec((1, xs.shape[1], xs.shape[2]), lambda s, c: (jnp.maximum(s - 1, 0), 0, 0)),
                pl.BlockSpec((1, xs.shape[1], xs.shape[2]), lambda s, c: (s, 0, 0)),
                pl.BlockSpec(
                    (1, xs.shape[1], xs.shape[2]), lambda s, c: (jnp.minimum(s + 1, shots - 1), 0, 0)
                ),
                pl.BlockSpec((1, xs.shape[1], xs.shape[2]), lambda s, c: (0, 0, 0)),
                pl.BlockSpec(weights.shape, lambda s, c: (0, 0, 0, 0, 0)),
                pl.BlockSpec((1, rows, lanes), lambda s, c: (s, 0, 0)),
            ],
            out_specs=pl.BlockSpec((1, rows, lanes), lambda s, c: (s, 0, 0)),
            scratch_shapes=[pltpu.VMEM((3 * xs.shape[2], 5 * lanes), weights.dtype)],
        ),
        out_shape=jax.ShapeDtypeStruct((shots, rows, lanes), jnp.bfloat16),
        compiler_params=pltpu.CompilerParams(vmem_limit_bytes=48 * 1024 * 1024),
        cost_estimate=pl.CostEstimate(
            flops=flops,
            transcendentals=0,
            bytes_accessed=(xs.size + low.size + high.size) * 2 + weights.size * 2 + 4 * shots * rows * lanes,
        ),
    )(scalars, low, xs, xs, xs, high, weights, flat)


def spread_kernel(
    scalars_ref, lo_ref, x0_ref, x1_ref, x2_ref, hi_ref, w_ref, res_ref, out_ref, rhs_ref, *, dilation, pairs
):
    s = pl.program_id(0)
    receiver_taps, shot_taps, time_taps, channels, _ = w_ref.shape

    @pl.when(s == 0)
    def _():
        zero = jnp.zeros((channels, channels), rhs_ref.dtype)
        for b in range(shot_taps):
            for e in range(time_taps + 1):
                row = (b * (time_taps + 1) + e) * channels
                for a in range(receiver_taps):
                    ahead = w_ref[a, b, e] if e < time_taps else zero
                    behind = w_ref[a, b, e - 1] if e >= 1 else zero
                    rhs_ref[pl.ds(row, channels), pl.ds(a * 2 * channels, 2 * channels)] = jnp.concatenate(
                        [ahead, behind], axis=1
                    )

    rows, lanes = out_ref.shape[1:]
    first_shot = jnp.where(s == 0, lo_ref[0], x0_ref[0])
    last_shot = jnp.where(s == pl.num_programs(0) - 1, hi_ref[0], x2_ref[0])
    lhs = jnp.concatenate([first_shot, x1_ref[0], last_shot], axis=1)
    spread = jnp.dot(lhs, rhs_ref[...], preferred_element_type=jnp.float32)
    total = None
    for a in range(5):
        part = spread[a * dilation * pairs : a * dilation * pairs + rows, a * lanes : (a + 1) * lanes]
        total = part if total is None else total + part
    first = scalars_ref[0] * (rows // pairs)
    receiver = first + lax.broadcasted_iota(jnp.int32, (rows, lanes), 0) // pairs
    live = receiver < scalars_ref[1 + s]
    value = res_ref[0].astype(jnp.float32) + jnp.maximum(total, 0.0)
    out_ref[0] = jnp.where(live, value, 0.0).astype(out_ref.dtype)


def halos(block, axis):
    count = lax.axis_size(axis)
    me = lax.axis_index(axis)
    forward = [(i, (i + 1) % count) for i in range(count)]
    backward = [((i + 1) % count, i) for i in range(count)]
    low = lax.ppermute(block[-1:], axis, forward)
    high = lax.ppermute(block[:1], axis, backward)
    low = jnp.where(me == 0, jnp.zeros_like(low), low)
    high = jnp.where(me == count - 1, jnp.zeros_like(high), high)
    return low, high


def stack_rows(volume, dilation, pairs):
    rows = volume.shape[1]
    phase = (jnp.arange(rows, dtype=jnp.int32) % pairs)[None, :, None]
    blank = jnp.zeros_like(volume[:, :1])
    before = jnp.concatenate([blank, volume[:, :-1]], axis=1)
    after = jnp.concatenate([volume[:, 1:], blank], axis=1)
    before = jnp.where(phase == 0, jnp.zeros_like(before), before)
    after = jnp.where(phase == pairs - 1, jnp.zeros_like(after), after)
    stacked = jnp.concatenate([before, volume, after], axis=2)
    margin = 2 * dilation * pairs
    return jnp.pad(stacked, ((0, 0), (margin, margin), (0, 0)))


def body(features, counts, first_weight, second_weight):
    receivers = features.shape[1]
    shot_local = features.shape[2]
    pairs = features.shape[3]
    lanes = features.shape[4]
    count = lax.axis_size("shot")
    me = lax.axis_index("shot")
    chosen = lax.dynamic_slice_in_dim(counts[:, 0], me * shot_local, shot_local)
    volume = jnp.transpose(features[0], (1, 0, 2, 3)).reshape(shot_local, receivers * pairs, lanes)
    alive = jnp.arange(receivers * pairs, dtype=jnp.int32)[None, :] // pairs < chosen[:, None]
    flat1 = volume * alive.astype(volume.dtype)[:, :, None]
    low1, high1 = halos(flat1, "shot")
    xs1 = stack_rows(flat1, 1, pairs)
    flat2 = spread_call(
        stack_rows(low1, 1, pairs), xs1, stack_rows(high1, 1, pairs), first_weight, flat1, chosen, 1, pairs
    )
    low2, high2 = halos(flat2, "shot")
    xs2 = stack_rows(flat2, 4, pairs)
    span = receivers // count
    whole = spread_call(
        stack_rows(low2, 4, pairs), xs2, stack_rows(high2, 4, pairs), second_weight, flat2, chosen, 4, pairs
    )
    arrived = []
    for shift in range(count):
        target = lax.rem(me + shift, count)
        piece = lax.dynamic_slice_in_dim(whole, target * span * pairs, span * pairs, axis=1)
        if shift:
            pairs_list = [(i, (i + shift) % count) for i in range(count)]
            piece = lax.ppermute(piece, "shot", pairs_list)
        arrived.append((shift, piece))
    by_shift = [piece for _, piece in sorted(arrived, key=lambda t: t[0])]
    ordered = jnp.concatenate(
        [lax.select_n(lax.rem(me - q + count, count), *by_shift) for q in range(count)], axis=0
    )
    ordered = ordered.reshape(count * shot_local, span, pairs, lanes)
    return jnp.transpose(ordered, (1, 0, 2, 3))[None]


def solution(mesh):
    placed = (P("cable", None, ("grp", "shot"), None, None), P("grp", "cable"), P(), P())
    return jax.shard_map(
        body,
        mesh=mesh,
        in_specs=placed,
        out_specs=P("cable", "shot", "grp", None, None),
        check_vma=False,
    )
```

```python
import functools

import jax
import jax.numpy as jnp
from jax import lax
from jax.experimental import pallas as pl
from jax.experimental.pallas import tpu as pltpu
from jax.sharding import PartitionSpec as P


def spread_call(low, xs, high, weights, flat, counts, dilation, pairs):
    shots, rows, lanes = flat.shape
    scalars = jnp.concatenate([jnp.zeros((1,), jnp.int32), counts])
    flops = 2 * shots * 3 * xs.shape[1] * xs.shape[2] * 5 * lanes
    return pl.pallas_call(
        functools.partial(spread_kernel, dilation=dilation, pairs=pairs),
        grid_spec=pltpu.PrefetchScalarGridSpec(
            num_scalar_prefetch=1,
            grid=(shots,),
            in_specs=[
                pl.BlockSpec((1, xs.shape[1], xs.shape[2]), lambda s, c: (0, 0, 0)),
                pl.BlockSpec((1, xs.shape[1], xs.shape[2]), lambda s, c: (jnp.maximum(s - 1, 0), 0, 0)),
                pl.BlockSpec((1, xs.shape[1], xs.shape[2]), lambda s, c: (s, 0, 0)),
                pl.BlockSpec(
                    (1, xs.shape[1], xs.shape[2]), lambda s, c: (jnp.minimum(s + 1, shots - 1), 0, 0)
                ),
                pl.BlockSpec((1, xs.shape[1], xs.shape[2]), lambda s, c: (0, 0, 0)),
                pl.BlockSpec(weights.shape, lambda s, c: (0, 0, 0, 0, 0)),
                pl.BlockSpec((1, rows, lanes), lambda s, c: (s, 0, 0)),
            ],
            out_specs=pl.BlockSpec((1, rows, lanes), lambda s, c: (s, 0, 0)),
            scratch_shapes=[pltpu.VMEM((3 * xs.shape[2], 5 * lanes), weights.dtype)],
        ),
        out_shape=jax.ShapeDtypeStruct((shots, rows, lanes), jnp.bfloat16),
        compiler_params=pltpu.CompilerParams(vmem_limit_bytes=24 * 1024 * 1024),
        cost_estimate=pl.CostEstimate(
            flops=flops,
            transcendentals=0,
            bytes_accessed=(xs.size + low.size + high.size) * 2 + weights.size * 2 + 4 * shots * rows * lanes,
        ),
    )(scalars, low, xs, xs, xs, high, weights, flat)


def spread_kernel(
    scalars_ref, lo_ref, x0_ref, x1_ref, x2_ref, hi_ref, w_ref, res_ref, out_ref, rhs_ref, *, dilation, pairs
):
    s = pl.program_id(0)
    receiver_taps, shot_taps, time_taps, channels, _ = w_ref.shape

    @pl.when(s == 0)
    def _():
        zero = jnp.zeros((channels, channels), rhs_ref.dtype)
        for b in range(shot_taps):
            for e in range(time_taps + 1):
                row = (b * (time_taps + 1) + e) * channels
                for a in range(receiver_taps):
                    ahead = w_ref[a, b, e] if e < time_taps else zero
                    behind = w_ref[a, b, e - 1] if e >= 1 else zero
                    rhs_ref[pl.ds(row, channels), pl.ds(a * 2 * channels, 2 * channels)] = jnp.concatenate(
                        [ahead, behind], axis=1
                    )

    rows, lanes = out_ref.shape[1:]
    first_shot = jnp.where(s == 0, lo_ref[0], x0_ref[0])
    last_shot = jnp.where(s == pl.num_programs(0) - 1, hi_ref[0], x2_ref[0])
    lhs = jnp.concatenate([first_shot, x1_ref[0], last_shot], axis=1)
    spread = jnp.dot(lhs, rhs_ref[...], preferred_element_type=jnp.float32)
    total = None
    for a in range(5):
        part = spread[a * dilation * pairs : a * dilation * pairs + rows, a * lanes : (a + 1) * lanes]
        total = part if total is None else total + part
    first = scalars_ref[0] * (rows // pairs)
    receiver = first + lax.broadcasted_iota(jnp.int32, (rows, lanes), 0) // pairs
    live = receiver < scalars_ref[1 + s]
    value = res_ref[0].astype(jnp.float32) + jnp.maximum(total, 0.0)
    out_ref[0] = jnp.where(live, value, 0.0).astype(out_ref.dtype)


def halos(block, axis):
    count = lax.axis_size(axis)
    me = lax.axis_index(axis)
    forward = [(i, (i + 1) % count) for i in range(count)]
    backward = [((i + 1) % count, i) for i in range(count)]
    low = lax.ppermute(block[-1:], axis, forward)
    high = lax.ppermute(block[:1], axis, backward)
    low = jnp.where(me == 0, jnp.zeros_like(low), low)
    high = jnp.where(me == count - 1, jnp.zeros_like(high), high)
    return low, high


def stack_rows(volume, dilation, pairs):
    rows = volume.shape[1]
    phase = (jnp.arange(rows, dtype=jnp.int32) % pairs)[None, :, None]
    blank = jnp.zeros_like(volume[:, :1])
    before = jnp.concatenate([blank, volume[:, :-1]], axis=1)
    after = jnp.concatenate([volume[:, 1:], blank], axis=1)
    before = jnp.where(phase == 0, jnp.zeros_like(before), before)
    after = jnp.where(phase == pairs - 1, jnp.zeros_like(after), after)
    stacked = jnp.concatenate([before, volume, after], axis=2)
    margin = 2 * dilation * pairs
    return jnp.pad(stacked, ((0, 0), (margin, margin), (0, 0)))


def body(features, counts, first_weight, second_weight):
    receivers = features.shape[1]
    shot_local = features.shape[2]
    pairs = features.shape[3]
    lanes = features.shape[4]
    count = lax.axis_size("shot")
    me = lax.axis_index("shot")
    chosen = lax.dynamic_slice_in_dim(counts[:, 0], me * shot_local, shot_local)
    volume = jnp.transpose(features[0], (1, 0, 2, 3)).reshape(shot_local, receivers * pairs, lanes)
    alive = jnp.arange(receivers * pairs, dtype=jnp.int32)[None, :] // pairs < chosen[:, None]
    flat1 = volume * alive.astype(volume.dtype)[:, :, None]
    low1, high1 = halos(flat1, "shot")
    xs1 = stack_rows(flat1, 1, pairs)
    flat2 = spread_call(
        stack_rows(low1, 1, pairs), xs1, stack_rows(high1, 1, pairs), first_weight, flat1, chosen, 1, pairs
    )
    low2, high2 = halos(flat2, "shot")
    xs2 = stack_rows(flat2, 4, pairs)
    span = receivers // count
    whole = spread_call(
        stack_rows(low2, 4, pairs), xs2, stack_rows(high2, 4, pairs), second_weight, flat2, chosen, 4, pairs
    )
    arrived = []
    for shift in range(count):
        target = lax.rem(me + shift, count)
        piece = lax.dynamic_slice_in_dim(whole, target * span * pairs, span * pairs, axis=1)
        if shift:
            pairs_list = [(i, (i + shift) % count) for i in range(count)]
            piece = lax.ppermute(piece, "shot", pairs_list)
        arrived.append((shift, piece))
    by_shift = [piece for _, piece in sorted(arrived, key=lambda t: t[0])]
    ordered = jnp.concatenate(
        [lax.select_n(lax.rem(me - q + count, count), *by_shift) for q in range(count)], axis=0
    )
    ordered = ordered.reshape(count * shot_local, span, pairs, lanes)
    return jnp.transpose(ordered, (1, 0, 2, 3))[None]


def solution(mesh):
    placed = (P("cable", None, ("grp", "shot"), None, None), P("grp", "cable"), P(), P())
    return jax.shard_map(
        body,
        mesh=mesh,
        in_specs=placed,
        out_specs=P("cable", "shot", "grp", None, None),
        check_vma=False,
    )
```

```python
import functools

import jax
import jax.numpy as jnp
from jax import lax
from jax.experimental import pallas as pl
from jax.experimental.pallas import tpu as pltpu
from jax.sharding import PartitionSpec as P


def spread_call(low, xs, high, weights, flat, counts, dilation, pairs, first=0, stride=1, steps=None):
    shots, rows, lanes = flat.shape
    steps = shots if steps is None else steps
    scalars = jnp.concatenate([jnp.zeros((1,), jnp.int32), counts])
    flops = 2 * steps * 3 * xs.shape[1] * xs.shape[2] * 5 * lanes
    return pl.pallas_call(
        functools.partial(spread_kernel, dilation=dilation, pairs=pairs, first=first, stride=stride, shots=shots),
        grid_spec=pltpu.PrefetchScalarGridSpec(
            num_scalar_prefetch=1,
            grid=(steps,),
            in_specs=[
                pl.BlockSpec((1, xs.shape[1], xs.shape[2]), lambda s, c: (0, 0, 0)),
                pl.BlockSpec(
                    (1, xs.shape[1], xs.shape[2]), lambda s, c: (jnp.maximum(first + s * stride - 1, 0), 0, 0)
                ),
                pl.BlockSpec((1, xs.shape[1], xs.shape[2]), lambda s, c: (first + s * stride, 0, 0)),
                pl.BlockSpec(
                    (1, xs.shape[1], xs.shape[2]),
                    lambda s, c: (jnp.minimum(first + s * stride + 1, shots - 1), 0, 0),
                ),
                pl.BlockSpec((1, xs.shape[1], xs.shape[2]), lambda s, c: (0, 0, 0)),
                pl.BlockSpec(weights.shape, lambda s, c: (0, 0, 0, 0, 0)),
                pl.BlockSpec((1, rows, lanes), lambda s, c: (first + s * stride, 0, 0)),
            ],
            out_specs=pl.BlockSpec((1, rows, lanes), lambda s, c: (s, 0, 0)),
            scratch_shapes=[pltpu.VMEM((3 * xs.shape[2], 5 * lanes), weights.dtype)],
        ),
        out_shape=jax.ShapeDtypeStruct((steps, rows, lanes), jnp.bfloat16),
        compiler_params=pltpu.CompilerParams(vmem_limit_bytes=24 * 1024 * 1024),
        cost_estimate=pl.CostEstimate(
            flops=flops,
            transcendentals=0,
            bytes_accessed=(xs.size + low.size + high.size) * 2 + weights.size * 2 + 4 * steps * rows * lanes,
        ),
    )(scalars, low, xs, xs, xs, high, weights, flat)


def spread_kernel(
    scalars_ref, lo_ref, x0_ref, x1_ref, x2_ref, hi_ref, w_ref, res_ref, out_ref, rhs_ref, *, dilation, pairs,
    first, stride, shots,
):
    step = pl.program_id(0)
    s = first + step * stride
    receiver_taps, shot_taps, time_taps, channels, _ = w_ref.shape

    @pl.when(step == 0)
    def _():
        zero = jnp.zeros((channels, channels), rhs_ref.dtype)
        for b in range(shot_taps):
            for e in range(time_taps + 1):
                row = (b * (time_taps + 1) + e) * channels
                for a in range(receiver_taps):
                    ahead = w_ref[a, b, e] if e < time_taps else zero
                    behind = w_ref[a, b, e - 1] if e >= 1 else zero
                    rhs_ref[pl.ds(row, channels), pl.ds(a * 2 * channels, 2 * channels)] = jnp.concatenate(
                        [ahead, behind], axis=1
                    )

    rows, lanes = out_ref.shape[1:]
    first_shot = jnp.where(s == 0, lo_ref[0], x0_ref[0])
    last_shot = jnp.where(s == shots - 1, hi_ref[0], x2_ref[0])
    lhs = jnp.concatenate([first_shot, x1_ref[0], last_shot], axis=1)
    spread = jnp.dot(lhs, rhs_ref[...], preferred_element_type=jnp.float32)
    total = None
    for a in range(5):
        part = spread[a * dilation * pairs : a * dilation * pairs + rows, a * lanes : (a + 1) * lanes]
        total = part if total is None else total + part
    first = scalars_ref[0] * (rows // pairs)
    receiver = first + lax.broadcasted_iota(jnp.int32, (rows, lanes), 0) // pairs
    live = receiver < scalars_ref[1 + s]
    value = res_ref[0].astype(jnp.float32) + jnp.maximum(total, 0.0)
    out_ref[0] = jnp.where(live, value, 0.0).astype(out_ref.dtype)


def halos(block, axis):
    count = lax.axis_size(axis)
    me = lax.axis_index(axis)
    forward = [(i, (i + 1) % count) for i in range(count)]
    backward = [((i + 1) % count, i) for i in range(count)]
    low = lax.ppermute(block[-1:], axis, forward)
    high = lax.ppermute(block[:1], axis, backward)
    low = jnp.where(me == 0, jnp.zeros_like(low), low)
    high = jnp.where(me == count - 1, jnp.zeros_like(high), high)
    return low, high


def stack_rows(volume, dilation, pairs):
    rows = volume.shape[1]
    phase = (jnp.arange(rows, dtype=jnp.int32) % pairs)[None, :, None]
    blank = jnp.zeros_like(volume[:, :1])
    before = jnp.concatenate([blank, volume[:, :-1]], axis=1)
    after = jnp.concatenate([volume[:, 1:], blank], axis=1)
    before = jnp.where(phase == 0, jnp.zeros_like(before), before)
    after = jnp.where(phase == pairs - 1, jnp.zeros_like(after), after)
    stacked = jnp.concatenate([before, volume, after], axis=2)
    margin = 2 * dilation * pairs
    return jnp.pad(stacked, ((0, 0), (margin, margin), (0, 0)))


def body(features, counts, first_weight, second_weight):
    receivers = features.shape[1]
    shot_local = features.shape[2]
    pairs = features.shape[3]
    lanes = features.shape[4]
    count = lax.axis_size("shot")
    me = lax.axis_index("shot")
    chosen = lax.dynamic_slice_in_dim(counts[:, 0], me * shot_local, shot_local)
    volume = jnp.transpose(features[0], (1, 0, 2, 3)).reshape(shot_local, receivers * pairs, lanes)
    alive = jnp.arange(receivers * pairs, dtype=jnp.int32)[None, :] // pairs < chosen[:, None]
    flat1 = volume * alive.astype(volume.dtype)[:, :, None]
    low1, high1 = halos(flat1, "shot")
    xs1 = stack_rows(flat1, 1, pairs)
    flat2 = spread_call(
        stack_rows(low1, 1, pairs), xs1, stack_rows(high1, 1, pairs), first_weight, flat1, chosen, 1, pairs
    )
    low2, high2 = halos(flat2, "shot")
    xs2 = stack_rows(flat2, 4, pairs)
    span = receivers // count
    halo2 = (stack_rows(low2, 4, pairs), xs2, stack_rows(high2, 4, pairs), second_weight, flat2, chosen, 4, pairs)
    inner = spread_call(xs2, xs2, xs2, *halo2[3:], 1, 1, shot_local - 2)
    edges = spread_call(*halo2, 0, shot_local - 1, 2)
    whole = jnp.concatenate([edges[:1], inner, edges[1:]], axis=0)
    arrived = []
    for shift in range(count):
        target = lax.rem(me + shift, count)
        piece = lax.dynamic_slice_in_dim(whole, target * span * pairs, span * pairs, axis=1)
        if shift:
            pairs_list = [(i, (i + shift) % count) for i in range(count)]
            piece = lax.ppermute(piece, "shot", pairs_list)
        arrived.append((shift, piece))
    by_shift = [piece for _, piece in sorted(arrived, key=lambda t: t[0])]
    ordered = jnp.concatenate(
        [lax.select_n(lax.rem(me - q + count, count), *by_shift) for q in range(count)], axis=0
    )
    ordered = ordered.reshape(count * shot_local, span, pairs, lanes)
    return jnp.transpose(ordered, (1, 0, 2, 3))[None]


def solution(mesh):
    placed = (P("cable", None, ("grp", "shot"), None, None), P("grp", "cable"), P(), P())
    return jax.shard_map(
        body,
        mesh=mesh,
        in_specs=placed,
        out_specs=P("cable", "shot", "grp", None, None),
        check_vma=False,
    )
```
